256 devices in a mesh: tile: 8 (over x, core), sub: 32 (over z, y).
Axes of the slice: x: 4, y: 4, z: 8, core: 2. Of those that a mesh axis runs over, the one named last changes fastest.
Arguments:
- parent: float32 [4, 91, 131072], P(None, None, ('tile', 'sub')), may hold values from -6 to 6
- parent_inverse: float32 [1024, 91, 91], P(('tile', 'sub'))
- nest: float32 [4, 91, 393216], P(None, None, ('tile', 'sub')), may hold values from -6 to 6
- nest_inverse: float32 [3072, 91, 91], P(('tile', 'sub'))
- interp: float32 [3072, 128, 128], P(('tile', 'sub'))
- relax: float32 [393216], P(('tile', 'sub')), may hold values from 0.2 to 0.9
- src_list: int32 [3072], P(('tile', 'sub')), may hold values from 0 to 127, as said below
- nest_live: int32 [3072], P(('tile', 'sub')), may hold values 0 or 1
- mixing: float32 [4], replicated, may hold values from 0.05 to 0.24
- nest_mixing: float32 [4], replicated, may hold values from 0.05 to 0.24
Outputs:
- parent_out: float32 [4, 91, 131072], P(None, None, ('tile', 'sub'))
- nest_out: float32 [4, 91, 393216], P(None, None, ('tile', 'sub'))
The draws below stay inside these ranges and needn't reach their ends.
Inputs may be any that keep to these rules, and one draw needn't show every extreme that they name: `src_list`: among the 12 entries of one device, no device of the face group owns more than 1 of the named parent blocks (a device owns 4 consecutive blocks), and in every device some owner is named exactly 1 times.
All inputs are finite; a program needn't handle non-finite values. No bound on the sum of `nest_live` on one device may be relied on, other than what follows from the above.
Results may differ from the reference program's by a relative error of at most 0.0001.
Values sent between devices are 32-bit elements; how exact they have to be, the bound alone decides.
No kernel may reach another device: no remote copies, remote signals or barrier semaphores. Data moves between devices by JAX's collectives and lax.ppermute only.
A program may use at most 128 MiB of HBM per device.

```python
import math
import jax
import jax.numpy as jnp
from jax import lax

F = 4
L = 91
BLK = 128
PB_DEV = 4
NB_DEV = 12
SUBSTEPS = 3
GROUP = 32
CAP = 1
NPB = 1024
NNB = 3072
NPC = 131072
NNC = 393216


def draw_src_list(key, part):
    rows_count = NNB // NB_DEV
    slots_count = GROUP * CAP
    first_key = jax.random.fold_in(key, 11)
    second_key = jax.random.fold_in(key, 12)
    owners_pool = jnp.arange(slots_count, dtype=jnp.int32) // CAP
    scores = jax.random.randint(first_key, (rows_count, slots_count), 0, 1 << 20)
    scores = scores * slots_count + jnp.arange(slots_count, dtype=jnp.int32)[None, :]
    order = jnp.argsort(scores, axis=1)[:, :NB_DEV]
    owners = owners_pool[order]
    local_block = jax.random.randint(second_key, (rows_count, NB_DEV), 0, PB_DEV)
    return (owners * PB_DEV + local_block).reshape(NNB).astype(jnp.int32)


def square_draw(key, count, size, diagonal, spread):
    identity = jnp.eye(size, dtype=jnp.float32)[None, :, :]
    noise = jax.random.normal(key, (count, size, size), jnp.float32)
    return diagonal * identity + spread * noise / jnp.sqrt(jnp.float32(size))


def draw_parent_inverse(key, part):
    return square_draw(jax.random.fold_in(key, 21), NPB, L, 0.8, 0.3)


def draw_nest_inverse(key, part):
    return square_draw(jax.random.fold_in(key, 22), NNB, L, 0.8, 0.3)


def draw_interp(key, part):
    return square_draw(jax.random.fold_in(key, 23), NNB, BLK, 0.6, 0.4)


def place_ends(entries, key, low, top_value):
    spot = [jax.random.randint(jax.random.fold_in(key, axis), (), 0, length) for axis, length in enumerate(entries.shape)]
    longest = entries.shape.index(max(entries.shape))
    beside = spot[:longest] + [(spot[longest] + 1) % entries.shape[longest]] + spot[longest + 1:]
    return entries.at[tuple(spot)].set(low).at[tuple(beside)].set(top_value)


def shard_levels(key, dims, cuts, least, largest):
    loudness = 1.0
    for dim, parts in cuts:
        steps = jax.random.uniform(jax.random.fold_in(jax.random.fold_in(key, 6), dim), (parts,), jnp.float32, least / len(cuts), largest / len(cuts))
        loudness = loudness * jnp.repeat(jnp.exp(steps), dims[dim] // parts).reshape((-1,) + (1,) * (len(dims) - 1 - dim))
    return loudness


def scatter_about(own_key, shape, deviation, most, shards=(), kind=jnp.bfloat16):
    gain = shard_levels(own_key, shape, shards, -0.22, 0.18) if shards else 1.0
    result = jax.random.normal(own_key, shape, jnp.float32) * deviation * gain
    return jnp.minimum(jnp.maximum(result, -most), most).astype(kind)


def setup_inputs(seed: int = 0) -> dict:
    key_of = jax.random.split(jax.random.key(seed), 11)
    return {
        "parent": scatter_about(key_of[0], (F, L, NPC), 1.0, 6.0, ((2, 256),), jnp.float32),
        "parent_inverse": draw_parent_inverse(jax.random.fold_in(key_of[10], 71), 0),
        "nest": scatter_about(key_of[2], (F, L, NNC), 1.0, 6.0, ((2, 256),), jnp.float32),
        "nest_inverse": draw_nest_inverse(jax.random.fold_in(key_of[10], 71), 0),
        "interp": draw_interp(jax.random.fold_in(key_of[10], 71), 0),
        "relax": jnp.clip(0.2 + 0.7 * jax.random.uniform(key_of[5], (NNC,), jnp.float32) ** shard_levels(key_of[5], (NNC,), ((0, 256),), -0.2, 0.2), 0.2, 0.9),
        "src_list": draw_src_list(jax.random.fold_in(key_of[10], 71), 0),
        "nest_live": place_ends((jax.random.randint(key_of[7], (NNB,), 0, 4) < 3).astype(jnp.int32), jax.random.fold_in(key_of[7], 1), 0, 1),
        "mixing": jnp.clip(jnp.exp(jax.random.uniform(key_of[8], (F,), jnp.float32, math.log(0.05), math.log(0.24))), 0.05, 0.24),
        "nest_mixing": jnp.clip(jnp.exp(jax.random.uniform(key_of[9], (F,), jnp.float32, math.log(0.05), math.log(0.24))), 0.05, 0.24),
    }


FEEDBACK = 0.25


def acoustic(values, inverse, coefs):
    lower = jnp.concatenate([values[..., :1], values[..., :-1]], axis=-1)
    upper = jnp.concatenate([values[..., 1:], values[..., -1:]], axis=-1)
    mixed = values + coefs[:, None, None, None] * (lower + upper - 2.0 * values)
    return jnp.einsum("jlm,fmjc->fljc", inverse, mixed, precision=lax.Precision.HIGHEST)


def reference(parent, parent_inverse, nest, nest_inverse, interp, relax, src_list, nest_live, mixing, nest_mixing):
    parent_total = parent_inverse.shape[0]
    nest_total = nest_inverse.shape[0]
    before = jnp.roll(parent, 1, axis=2)
    after = jnp.roll(parent, -1, axis=2)
    smoothed = parent + mixing[:, None, None] * (before + after - 2.0 * parent)
    shaped = smoothed.reshape(F, L, parent_total, BLK)
    stepped = jnp.einsum("klm,fmkc->flkc", parent_inverse, shaped, precision=lax.Precision.HIGHEST)
    block_ids = jnp.arange(nest_total, dtype=jnp.int32)
    source = ((block_ids // (NB_DEV * GROUP)) * (PB_DEV * GROUP) + src_list).astype(jnp.int32)
    fetched = jnp.take(stepped, source, axis=2)
    boundary = jnp.einsum("jic,fljc->flji", interp, fetched, precision=lax.Precision.HIGHEST)
    state = nest.reshape(F, L, nest_total, BLK)
    weights = relax.reshape(nest_total, BLK)
    forced = state + weights * (boundary - state)
    for substep in range(SUBSTEPS):
        forced = acoustic(forced, nest_inverse, nest_mixing)
    alive = nest_live == 1
    nest_out = jnp.where(alive[None, None, :, None], forced, state)
    live_float = alive.astype(jnp.float32)
    restricted = jnp.einsum("jic,flji->fljc", interp, forced, precision=lax.Precision.HIGHEST) * live_float[None, None, :, None]
    summed = jnp.zeros(stepped.shape, jnp.float32).at[:, :, source, :].add(restricted)
    counts = jnp.zeros((parent_total,), jnp.float32).at[source].add(live_float)
    parent_out = stepped + FEEDBACK * (summed - counts[None, None, :, None] * stepped)
    return parent_out.reshape(F, L, parent_total * BLK), nest_out.reshape(F, L, nest_total * BLK)
```

```python
import jax
import jax.numpy as jnp
import numpy as np
from jax import lax
from jax.sharding import Mesh
from jax.sharding import PartitionSpec as P

SUBSTEPS = 3


FEEDBACK = 0.25

HIGH = lax.Precision.HIGHEST


def with_halo(block, sides, width):
    for axis, dim in sides:
        count = lax.axis_size(axis)
        forward = [(i, i + 1) for i in range(count - 1)]
        forward.append((count - 1, 0))
        backward = [(target, source) for source, target in forward]
        low = lax.ppermute(
            lax.slice_in_dim(block, block.shape[dim] - width, None, axis=dim), axis, forward
        )
        high = lax.ppermute(lax.slice_in_dim(block, 0, width, axis=dim), axis, backward)
        block = jnp.concatenate([low, block, high], axis=dim)
    return block


def acoustic(values, inverse, coefs):
    lower = jnp.concatenate([values[..., :1], values[..., :-1]], axis=-1)
    upper = jnp.concatenate([values[..., 1:], values[..., -1:]], axis=-1)
    mixed = values + coefs[:, None, None, None] * (lower + upper - 2.0 * values)
    return jnp.einsum("jlm,fmjc->fljc", inverse, mixed, precision=HIGH)


def body(
    parent,
    parent_inverse,
    nest,
    nest_inverse,
    interp,
    relax,
    src_list,
    nest_live,
    mixing,
    nest_mixing,
):
    fields, levels, parent_cols = parent.shape
    parent_count = parent_inverse.shape[0]
    nest_count = nest_inverse.shape[0]
    width = interp.shape[1]
    zs = lax.axis_size("z")
    ys = lax.axis_size("y")
    my_y = lax.axis_index("y")

    padded = with_halo(parent, ((("tile", "z", "y"), 2),), 1)
    smoothed = parent + mixing[:, None, None] * (
        padded[:, :, :-2] + padded[:, :, 2:] - 2.0 * parent
    )
    shaped = smoothed.reshape(fields, levels, parent_count, width)
    stepped = jnp.einsum("klm,fmkc->kflc", parent_inverse, shaped, precision=HIGH)

    owner = src_list // parent_count
    local = src_list % parent_count
    owner_z = owner // ys
    owner_y = owner % ys

    row_lists = lax.all_gather(src_list, "y", axis=0, tiled=False)
    row_owner = row_lists // parent_count
    row_local = row_lists % parent_count
    column = jnp.arange(zs, dtype=jnp.int32) * ys + my_y
    hit = row_owner[:, :, None] == column[None, None, :]
    pick = jnp.max(jnp.where(hit, row_local[:, :, None], 0), axis=1)

    gathered = lax.all_gather(stepped, "z", axis=0, tiled=True)
    index = (jnp.arange(zs, dtype=jnp.int32)[None, :] * parent_count + pick).reshape(-1)
    outgoing = jnp.take(gathered, index, axis=0)
    arrived = lax.all_to_all(outgoing, "y", split_axis=0, concat_axis=0, tiled=True)
    slot = owner_y * zs + owner_z
    fetched = jnp.take(arrived, slot, axis=0)

    state = nest.reshape(fields, levels, nest_count, width)
    weights = relax.reshape(nest_count, width)
    alive = nest_live == 1
    live_float = alive.astype(jnp.float32)
    boundary = jnp.einsum("jic,jflc->flji", interp, fetched, precision=HIGH)
    forced = state + weights * (boundary - state)
    for substep in range(SUBSTEPS):
        forced = acoustic(forced, nest_inverse, nest_mixing)
    nest_out = jnp.where(alive[None, None, :, None], forced, state)
    restricted = jnp.einsum("jic,flji->jflc", interp, forced, precision=HIGH)
    change = live_float[:, None, None, None] * (restricted - fetched)

    slots = jnp.arange(ys * zs, dtype=jnp.int32)
    gather_back = (slot[None, :] == slots[:, None]).astype(jnp.float32)
    returning = jnp.einsum("qj,jflc->qflc", gather_back, change, precision=HIGH)
    landed = lax.all_to_all(returning, "y", split_axis=0, concat_axis=0, tiled=True)
    landed = landed.reshape((ys, zs) + landed.shape[1:])
    place = (pick[:, :, None] == jnp.arange(parent_count, dtype=jnp.int32)[None, None, :]).astype(
        jnp.float32
    )
    partial = jnp.einsum("yzk,yzflc->zkflc", place, landed, precision=HIGH)
    partial = partial.reshape((zs * parent_count,) + partial.shape[2:])
    summed = lax.psum_scatter(partial, "z", scatter_dimension=0, tiled=True)
    parent_out = stepped + FEEDBACK * summed
    parent_out = jnp.transpose(parent_out, (1, 2, 0, 3))
    return (
        parent_out.reshape(fields, levels, parent_cols),
        nest_out.reshape(fields, levels, nest_count * width),
    )


def split_mesh(mesh):
    devices = mesh.devices
    tiles, subs = devices.shape
    first = devices[0]
    try:
        ys = len({d.coords[1] for d in first})
    except Exception:
        ys = 4
    if subs % ys:
        ys = 1
    return Mesh(devices.reshape(tiles, subs // ys, ys), ("tile", "z", "y"))


def solution(mesh):
    inner = split_mesh(mesh)
    cols = P(None, None, ("tile", "z", "y"))
    rows = P(("tile", "z", "y"), None, None)
    flat = P(("tile", "z", "y"))
    in_specs = (cols, rows, cols, rows, rows, flat, flat, flat, P(), P())
    out_specs = (cols, cols)
    return jax.shard_map(body, mesh=inner, in_specs=in_specs, out_specs=out_specs, check_vma=False)
```

```python
import jax
import jax.numpy as jnp
import numpy as np
from jax import lax
from jax.sharding import Mesh
from jax.sharding import PartitionSpec as P

SUBSTEPS = 3


FEEDBACK = 0.25

HIGH = lax.Precision.HIGHEST


def with_halo(block, sides, width):
    for axis, dim in sides:
        count = lax.axis_size(axis)
        forward = [(i, i + 1) for i in range(count - 1)]
        forward.append((count - 1, 0))
        backward = [(target, source) for source, target in forward]
        low = lax.ppermute(
            lax.slice_in_dim(block, block.shape[dim] - width, None, axis=dim), axis, forward
        )
        high = lax.ppermute(lax.slice_in_dim(block, 0, width, axis=dim), axis, backward)
        block = jnp.concatenate([low, block, high], axis=dim)
    return block


def acoustic(values, inverse, coefs):
    lower = jnp.concatenate([values[..., :1], values[..., :-1]], axis=-1)
    upper = jnp.concatenate([values[..., 1:], values[..., -1:]], axis=-1)
    mixed = values + coefs[:, None, None, None] * (lower + upper - 2.0 * values)
    return jnp.einsum("jlm,fmjc->fljc", inverse, mixed, precision=HIGH)


def body(
    parent,
    parent_inverse,
    nest,
    nest_inverse,
    interp,
    relax,
    src_list,
    nest_live,
    mixing,
    nest_mixing,
):
    fields, levels, parent_cols = parent.shape
    parent_count = parent_inverse.shape[0]
    nest_count = nest_inverse.shape[0]
    width = interp.shape[1]
    zs = lax.axis_size("z")
    ys = lax.axis_size("y")
    my_y = lax.axis_index("y")

    padded = with_halo(parent, ((("tile", "z", "y"), 2),), 1)
    smoothed_all = parent + mixing[:, None, None] * (
        padded[:, :, :-2] + padded[:, :, 2:] - 2.0 * parent
    )

    owner = src_list // parent_count
    owner_z = owner // ys
    owner_y = owner % ys
    slot = owner_y * zs + owner_z

    row_lists = lax.all_gather(src_list, "y", axis=0, tiled=False)
    row_owner = row_lists // parent_count
    row_local = row_lists % parent_count
    column = jnp.arange(zs, dtype=jnp.int32) * ys + my_y
    hit = row_owner[:, :, None] == column[None, None, :]
    pick = jnp.max(jnp.where(hit, row_local[:, :, None], 0), axis=1)
    index = (jnp.arange(zs, dtype=jnp.int32)[None, :] * parent_count + pick).reshape(-1)

    slots = jnp.arange(ys * zs, dtype=jnp.int32)
    gather_back = (slot[None, :] == slots[:, None]).astype(jnp.float32)
    place = pick[:, :, None] == jnp.arange(parent_count, dtype=jnp.int32)[None, None, :]

    weights = relax.reshape(nest_count, width)
    alive = nest_live == 1
    live_float = alive.astype(jnp.float32)

    parent_parts = []
    nest_parts = []
    carry = None
    back = None
    for field in range(fields):
        shaped = smoothed_all[field].reshape(levels, parent_count, width)
        stepped = jnp.einsum("klm,mkc->klc", parent_inverse, shaped, precision=HIGH)
        if carry is not None:
            carry, stepped = lax.optimization_barrier((carry, stepped))
        gathered = lax.all_gather(stepped, "z", axis=0, tiled=True)
        outgoing = jnp.take(gathered, index, axis=0)
        arrived = lax.all_to_all(outgoing, "y", split_axis=0, concat_axis=0, tiled=True)
        fetched = jnp.take(arrived, slot, axis=0)
        carry = outgoing

        state = nest[field].reshape(levels, nest_count, width)
        coef = nest_mixing[field]
        boundary = jnp.einsum("jic,jlc->lji", interp, fetched, precision=HIGH)
        forced = state + weights * (boundary - state)
        for substep in range(SUBSTEPS):
            lower = jnp.concatenate([forced[..., :1], forced[..., :-1]], axis=-1)
            upper = jnp.concatenate([forced[..., 1:], forced[..., -1:]], axis=-1)
            mixed = forced + coef * (lower + upper - 2.0 * forced)
            forced = jnp.einsum("jlm,mjc->ljc", nest_inverse, mixed, precision=HIGH)
        nest_out = jnp.where(alive[None, :, None], forced, state)
        restricted = jnp.einsum("jic,lji->jlc", interp, forced, precision=HIGH)
        change = live_float[:, None, None] * (restricted - fetched)

        returning = jnp.einsum("qj,jlc->qlc", gather_back, change, precision=HIGH)
        if back is not None:
            back, returning = lax.optimization_barrier((back, returning))
        landed = lax.all_to_all(returning, "y", split_axis=0, concat_axis=0, tiled=True)
        landed = landed.reshape((ys, zs) + landed.shape[1:])
        partial = jnp.sum(
            jnp.where(place[:, :, :, None, None], landed[:, :, None], 0.0), axis=0
        )
        partial = partial.reshape((zs * parent_count,) + partial.shape[2:])
        back = partial
        summed = lax.psum_scatter(partial, "z", scatter_dimension=0, tiled=True)
        parent_out = stepped + FEEDBACK * summed
        parent_parts.append(jnp.transpose(parent_out, (1, 0, 2)))
        nest_parts.append(nest_out)
    parent_out = jnp.stack(parent_parts, axis=0)
    nest_out = jnp.stack(nest_parts, axis=0)
    return (
        parent_out.reshape(fields, levels, parent_cols),
        nest_out.reshape(fields, levels, nest_count * width),
    )


def split_mesh(mesh):
    devices = mesh.devices
    tiles, subs = devices.shape
    first = devices[0]
    try:
        ys = len({d.coords[1] for d in first})
    except Exception:
        ys = 4
    if subs % ys:
        ys = 1
    return Mesh(devices.reshape(tiles, subs // ys, ys), ("tile", "z", "y"))


def solution(mesh):
    inner = split_mesh(mesh)
    cols = P(None, None, ("tile", "z", "y"))
    rows = P(("tile", "z", "y"), None, None)
    flat = P(("tile", "z", "y"))
    in_specs = (cols, rows, cols, rows, rows, flat, flat, flat, P(), P())
    out_specs = (cols, cols)
    return jax.shard_map(body, mesh=inner, in_specs=in_specs, out_specs=out_specs, check_vma=False)
```

```python
import jax
import jax.numpy as jnp
from jax import lax
from jax.sharding import PartitionSpec as P

SUBSTEPS = 3


FEEDBACK = 0.25

HIGH = lax.Precision.HIGHEST


def with_halo(block, sides, width):
    for axis, dim in sides:
        count = lax.axis_size(axis)
        forward = [(i, i + 1) for i in range(count - 1)]
        forward.append((count - 1, 0))
        backward = [(target, source) for source, target in forward]
        low = lax.ppermute(
            lax.slice_in_dim(block, block.shape[dim] - width, None, axis=dim), axis, forward
        )
        high = lax.ppermute(lax.slice_in_dim(block, 0, width, axis=dim), axis, backward)
        block = jnp.concatenate([low, block, high], axis=dim)
    return block


def body(
    parent,
    parent_inverse,
    nest,
    nest_inverse,
    interp,
    relax,
    src_list,
    nest_live,
    mixing,
    nest_mixing,
):
    fields, levels, parent_cols = parent.shape
    parent_count = parent_inverse.shape[0]
    nest_count = nest_inverse.shape[0]
    width = interp.shape[1]
    group = lax.axis_size("sub")

    padded = with_halo(parent, ((("tile", "sub"), 2),), 1)
    smoothed_all = parent + mixing[:, None, None] * (
        padded[:, :, :-2] + padded[:, :, 2:] - 2.0 * parent
    )

    owner = src_list // parent_count
    local = src_list % parent_count
    peers = jnp.arange(group, dtype=jnp.int32)
    named = owner[None, :] == peers[:, None]
    want = jnp.max(jnp.where(named, local[None, :], -1), axis=1)
    wanted = lax.all_to_all(want, "sub", split_axis=0, concat_axis=0, tiled=True)
    send_index = jnp.maximum(wanted, 0)
    gather_back = named.astype(jnp.float32)
    blocks = jnp.arange(parent_count, dtype=jnp.int32)
    place = (wanted[None, :] == blocks[:, None]).astype(jnp.float32)

    weights = relax.reshape(nest_count, width)
    alive = nest_live == 1
    live_float = alive.astype(jnp.float32)

    parent_parts = []
    nest_parts = []
    for field in range(fields):
        shaped = smoothed_all[field].reshape(levels, parent_count, width)
        stepped = jnp.einsum("klm,mkc->klc", parent_inverse, shaped, precision=HIGH)
        outgoing = jnp.take(stepped, send_index, axis=0)
        arrived = lax.all_to_all(outgoing, "sub", split_axis=0, concat_axis=0, tiled=True)
        fetched = jnp.take(arrived, owner, axis=0)

        state = nest[field].reshape(levels, nest_count, width)
        coef = nest_mixing[field]
        boundary = jnp.einsum("jic,jlc->lji", interp, fetched, precision=HIGH)
        forced = state + weights * (boundary - state)
        for substep in range(SUBSTEPS):
            lower = jnp.concatenate([forced[..., :1], forced[..., :-1]], axis=-1)
            upper = jnp.concatenate([forced[..., 1:], forced[..., -1:]], axis=-1)
            mixed = forced + coef * (lower + upper - 2.0 * forced)
            forced = jnp.einsum("jlm,mjc->ljc", nest_inverse, mixed, precision=HIGH)
        nest_out = jnp.where(alive[None, :, None], forced, state)
        restricted = jnp.einsum("jic,lji->jlc", interp, forced, precision=HIGH)
        change = live_float[:, None, None] * (restricted - fetched)

        returning = jnp.einsum("oj,jlc->olc", gather_back, change, precision=HIGH)
        landed = lax.all_to_all(returning, "sub", split_axis=0, concat_axis=0, tiled=True)
        summed = jnp.einsum("kg,glc->klc", place, landed, precision=HIGH)
        parent_out = stepped + FEEDBACK * summed
        parent_parts.append(jnp.transpose(parent_out, (1, 0, 2)).reshape(levels, parent_cols))
        nest_parts.append(nest_out.reshape(levels, nest_count * width))
    return jnp.stack(parent_parts, axis=0), jnp.stack(nest_parts, axis=0)


def solution(mesh):
    cols = P(None, None, ("tile", "sub"))
    rows = P(("tile", "sub"), None, None)
    flat = P(("tile", "sub"))
    in_specs = (cols, rows, cols, rows, rows, flat, flat, flat, P(), P())
    out_specs = (cols, cols)
    return jax.shard_map(body, mesh=mesh, in_specs=in_specs, out_specs=out_specs, check_vma=False)
```

```python
import jax
import jax.numpy as jnp
from jax import lax
from jax.sharding import PartitionSpec as P

SUBSTEPS = 3


FEEDBACK = 0.25

HIGH = lax.Precision.HIGHEST


def with_halo(block, sides, width):
    for axis, dim in sides:
        count = lax.axis_size(axis)
        forward = [(i, i + 1) for i in range(count - 1)]
        forward.append((count - 1, 0))
        backward = [(target, source) for source, target in forward]
        low = lax.ppermute(
            lax.slice_in_dim(block, block.shape[dim] - width, None, axis=dim), axis, forward
        )
        high = lax.ppermute(lax.slice_in_dim(block, 0, width, axis=dim), axis, backward)
        block = jnp.concatenate([low, block, high], axis=dim)
    return block


def body(
    parent,
    parent_inverse,
    nest,
    nest_inverse,
    interp,
    relax,
    src_list,
    nest_live,
    mixing,
    nest_mixing,
):
    fields, levels, parent_cols = parent.shape
    parent_count = parent_inverse.shape[0]
    nest_count = nest_inverse.shape[0]
    width = interp.shape[1]
    group = lax.axis_size("sub")

    padded = with_halo(parent, ((("tile", "sub"), 2),), 1)
    smoothed_all = parent + mixing[:, None, None] * (
        padded[:, :, :-2] + padded[:, :, 2:] - 2.0 * parent
    )

    owner = src_list // parent_count
    local = src_list % parent_count
    peers = jnp.arange(group, dtype=jnp.int32)
    named = owner[None, :] == peers[:, None]
    want = jnp.max(jnp.where(named, local[None, :], -1), axis=1)
    wanted = lax.all_to_all(want, "sub", split_axis=0, concat_axis=0, tiled=True)
    send_index = jnp.maximum(wanted, 0)
    gather_back = named.astype(jnp.float32)
    blocks = jnp.arange(parent_count, dtype=jnp.int32)
    place = (wanted[None, :] == blocks[:, None]).astype(jnp.float32)

    weights = relax.reshape(nest_count, width)
    alive = nest_live == 1
    live_float = alive.astype(jnp.float32)

    shaped = smoothed_all.reshape(fields, levels, parent_count, width)
    stepped = jnp.einsum("klm,fmkc->kflc", parent_inverse, shaped, precision=HIGH)
    outgoing = jnp.take(stepped, send_index, axis=0)
    arrived = lax.all_to_all(outgoing, "sub", split_axis=0, concat_axis=0, tiled=True)
    fetched = jnp.take(arrived, owner, axis=0)

    state = nest.reshape(fields, levels, nest_count, width)
    boundary = jnp.einsum("jic,jflc->flji", interp, fetched, precision=HIGH)
    forced = state + weights * (boundary - state)
    coef = nest_mixing[:, None, None, None]
    for substep in range(SUBSTEPS):
        lower = jnp.concatenate([forced[..., :1], forced[..., :-1]], axis=-1)
        upper = jnp.concatenate([forced[..., 1:], forced[..., -1:]], axis=-1)
        mixed = forced + coef * (lower + upper - 2.0 * forced)
        forced = jnp.einsum("jlm,fmjc->fljc", nest_inverse, mixed, precision=HIGH)
    nest_out = jnp.where(alive[None, None, :, None], forced, state)
    restricted = jnp.einsum("jic,flji->jflc", interp, forced, precision=HIGH)
    change = live_float[:, None, None, None] * (restricted - fetched)

    returning = jnp.einsum("oj,jflc->oflc", gather_back, change, precision=HIGH)
    landed = lax.all_to_all(returning, "sub", split_axis=0, concat_axis=0, tiled=True)
    summed = jnp.einsum("kg,gflc->kflc", place, landed, precision=HIGH)
    parent_out = stepped + FEEDBACK * summed
    parent_out = jnp.transpose(parent_out, (1, 2, 0, 3)).reshape(fields, levels, parent_cols)
    return parent_out, nest_out.reshape(fields, levels, nest_count * width)


def solution(mesh):
    cols = P(None, None, ("tile", "sub"))
    rows = P(("tile", "sub"), None, None)
    flat = P(("tile", "sub"))
    in_specs = (cols, rows, cols, rows, rows, flat, flat, flat, P(), P())
    out_specs = (cols, cols)
    return jax.shard_map(body, mesh=mesh, in_specs=in_specs, out_specs=out_specs, check_vma=False)
```

```python
import jax
import jax.numpy as jnp
from jax import lax
from jax.experimental import pallas as pl
from jax.experimental.pallas import tpu as pltpu
from jax.sharding import PartitionSpec as P

SUBSTEPS = 3


FEEDBACK = 0.25

HIGH = lax.Precision.HIGHEST


def with_halo(block, sides, width):
    for axis, dim in sides:
        count = lax.axis_size(axis)
        forward = [(i, i + 1) for i in range(count - 1)]
        forward.append((count - 1, 0))
        backward = [(target, source) for source, target in forward]
        low = lax.ppermute(
            lax.slice_in_dim(block, block.shape[dim] - width, None, axis=dim), axis, forward
        )
        high = lax.ppermute(lax.slice_in_dim(block, 0, width, axis=dim), axis, backward)
        block = jnp.concatenate([low, block, high], axis=dim)
    return block


def nest_kernel(live_ref, coef_ref, fetched_ref, nest_ref, relax_ref, inv_ref, interp_ref, out_ref, change_ref):
    j = pl.program_id(0)
    live = live_ref[j] == 1
    fields, levels, width = nest_ref.shape
    weights = relax_ref[0]
    inverse = inv_ref[0]
    weights_ip = interp_ref[0]
    lane = lax.broadcasted_iota(jnp.int32, (levels, width), 1)
    for field in range(fields):
        fetched = fetched_ref[0, field]
        state = nest_ref[field]
        boundary = lax.dot_general(fetched, weights_ip, (((1,), (1,)), ((), ())), precision=HIGH,
                                   preferred_element_type=jnp.float32)
        forced = state + weights * (boundary - state)
        coef = coef_ref[field]
        for substep in range(SUBSTEPS):
            lower = jnp.where(lane == 0, forced, pltpu.roll(forced, 1, 1))
            upper = jnp.where(lane == width - 1, forced, pltpu.roll(forced, width - 1, 1))
            mixed = forced + coef * (lower + upper - 2.0 * forced)
            forced = jnp.dot(inverse, mixed, precision=HIGH, preferred_element_type=jnp.float32)
        out_ref[field] = jnp.where(live, forced, state)
        restricted = jnp.dot(forced, weights_ip, precision=HIGH, preferred_element_type=jnp.float32)
        change_ref[0, field] = jnp.where(live, restricted - fetched, 0.0)

def nest_step(nest_live, nest_mixing, fetched, nest, relax, nest_inverse, interp):
    count, fields, levels, width = fetched.shape
    grid_spec = pltpu.PrefetchScalarGridSpec(
        num_scalar_prefetch=1,
        grid=(count,),
        in_specs=[
            pl.BlockSpec(memory_space=pltpu.SMEM),
            pl.BlockSpec((1, fields, levels, width), lambda j, live: (j, 0, 0, 0)),
            pl.BlockSpec((fields, levels, width), lambda j, live: (0, 0, j)),
            pl.BlockSpec((1, 1, width), lambda j, live: (j, 0, 0)),
            pl.BlockSpec((1, levels, levels), lambda j, live: (j, 0, 0)),
            pl.BlockSpec((1, width, width), lambda j, live: (j, 0, 0)),
        ],
        out_specs=[
            pl.BlockSpec((fields, levels, width), lambda j, live: (0, 0, j)),
            pl.BlockSpec((1, fields, levels, width), lambda j, live: (j, 0, 0, 0)),
        ],
    )
    return pl.pallas_call(
        nest_kernel,
        grid_spec=grid_spec,
        out_shape=[jax.ShapeDtypeStruct(nest.shape, jnp.float32), jax.ShapeDtypeStruct(fetched.shape, jnp.float32)],
    )(nest_live, nest_mixing, fetched, nest, relax.reshape(count, 1, width), nest_inverse, interp)


def body(
    parent,
    parent_inverse,
    nest,
    nest_inverse,
    interp,
    relax,
    src_list,
    nest_live,
    mixing,
    nest_mixing,
):
    fields, levels, parent_cols = parent.shape
    parent_count = parent_inverse.shape[0]
    nest_count = nest_inverse.shape[0]
    width = interp.shape[1]
    group = lax.axis_size("sub")

    padded = with_halo(parent, ((("tile", "sub"), 2),), 1)
    smoothed_all = parent + mixing[:, None, None] * (
        padded[:, :, :-2] + padded[:, :, 2:] - 2.0 * parent
    )

    owner = src_list // parent_count
    local = src_list % parent_count
    peers = jnp.arange(group, dtype=jnp.int32)
    named = owner[None, :] == peers[:, None]
    want = jnp.max(jnp.where(named, local[None, :], -1), axis=1)
    wanted = lax.all_to_all(want, "sub", split_axis=0, concat_axis=0, tiled=True)
    send_index = jnp.maximum(wanted, 0)
    gather_back = named.astype(jnp.float32)
    blocks = jnp.arange(parent_count, dtype=jnp.int32)
    place = (wanted[None, :] == blocks[:, None]).astype(jnp.float32)

    shaped = smoothed_all.reshape(fields, levels, parent_count, width)
    stepped = jnp.einsum("klm,fmkc->kflc", parent_inverse, shaped, precision=HIGH)
    outgoing = jnp.take(stepped, send_index, axis=0)
    arrived = lax.all_to_all(outgoing, "sub", split_axis=0, concat_axis=0, tiled=True)
    fetched = jnp.take(arrived, owner, axis=0)

    nest_out, change = nest_step(nest_live, nest_mixing, fetched, nest, relax, nest_inverse, interp)

    returning = jnp.einsum("oj,jflc->oflc", gather_back, change, precision=HIGH)
    landed = lax.all_to_all(returning, "sub", split_axis=0, concat_axis=0, tiled=True)
    summed = jnp.einsum("kg,gflc->kflc", place, landed, precision=HIGH)
    parent_out = stepped + FEEDBACK * summed
    parent_out = jnp.transpose(parent_out, (1, 2, 0, 3)).reshape(fields, levels, parent_cols)
    return parent_out, nest_out


def solution(mesh):
    cols = P(None, None, ("tile", "sub"))
    rows = P(("tile", "sub"), None, None)
    flat = P(("tile", "sub"))
    in_specs = (cols, rows, cols, rows, rows, flat, flat, flat, P(), P())
    out_specs = (cols, cols)
    return jax.shard_map(body, mesh=mesh, in_specs=in_specs, out_specs=out_specs, check_vma=False)
```

```python
import jax
import jax.numpy as jnp
from jax import lax
from jax.experimental import pallas as pl
from jax.experimental.pallas import tpu as pltpu
from jax.sharding import PartitionSpec as P

SUBSTEPS = 3


FEEDBACK = 0.25

HIGH = lax.Precision.HIGHEST


def with_halo(block, sides, width):
    for axis, dim in sides:
        count = lax.axis_size(axis)
        forward = [(i, i + 1) for i in range(count - 1)]
        forward.append((count - 1, 0))
        backward = [(target, source) for source, target in forward]
        low = lax.ppermute(
            lax.slice_in_dim(block, block.shape[dim] - width, None, axis=dim), axis, forward
        )
        high = lax.ppermute(lax.slice_in_dim(block, 0, width, axis=dim), axis, backward)
        block = jnp.concatenate([low, block, high], axis=dim)
    return block


def dot3(a, b, dims):
    ah = a.astype(jnp.bfloat16)
    al = (a - ah.astype(jnp.float32)).astype(jnp.bfloat16)
    bh = b.astype(jnp.bfloat16)
    bl = (b - bh.astype(jnp.float32)).astype(jnp.bfloat16)
    f = lambda x, y: lax.dot_general(x, y, dims, preferred_element_type=jnp.float32)
    return f(ah, bh) + (f(ah, bl) + f(al, bh))

ROWS = (((1,), (0,)), ((), ()))
COLS = (((1,), (1,)), ((), ()))

def nest_kernel(live_ref, coef_ref, fetched_ref, nest_ref, relax_ref, inv_ref, interp_ref, out_ref, change_ref):
    group, fields, levels, width = fetched_ref.shape
    lane = lax.broadcasted_iota(jnp.int32, (levels, fields * width), 1) % width
    coef = jnp.concatenate(
        [jnp.full((1, width), coef_ref[field], jnp.float32) for field in range(fields)], axis=1
    )
    for g in range(group):
        live = live_ref[pl.program_id(0) * group + g] == 1
        cols = slice(g * width, (g + 1) * width)
        weights = relax_ref[g]
        inverse = inv_ref[g]
        weights_ip = interp_ref[g]
        states = []
        forced = []
        for field in range(fields):
            state = nest_ref[field, :, cols]
            boundary = dot3(fetched_ref[g, field], weights_ip, COLS)
            states.append(state)
            forced.append(state + weights * (boundary - state))
        forced = jnp.concatenate(forced, axis=1)
        for substep in range(SUBSTEPS):
            lower = jnp.where(lane == 0, forced, pltpu.roll(forced, 1, 1))
            upper = jnp.where(lane == width - 1, forced, pltpu.roll(forced, fields * width - 1, 1))
            mixed = forced + coef * (lower + upper - 2.0 * forced)
            forced = dot3(inverse, mixed, ROWS)
        for field in range(fields):
            part = forced[:, field * width:(field + 1) * width]
            out_ref[field, :, cols] = jnp.where(live, part, states[field])
            restricted = dot3(part, weights_ip, ROWS)
            change_ref[g, field] = jnp.where(live, restricted - fetched_ref[g, field], 0.0)


def nest_step(nest_live, nest_mixing, fetched, nest, relax, nest_inverse, interp, group=4):
    count, fields, levels, width = fetched.shape
    grid_spec = pltpu.PrefetchScalarGridSpec(
        num_scalar_prefetch=1,
        grid=(count // group,),
        in_specs=[
            pl.BlockSpec(memory_space=pltpu.SMEM),
            pl.BlockSpec((group, fields, levels, width), lambda j, live: (j, 0, 0, 0)),
            pl.BlockSpec((fields, levels, group * width), lambda j, live: (0, 0, j)),
            pl.BlockSpec((group, 1, width), lambda j, live: (j, 0, 0)),
            pl.BlockSpec((group, levels, levels), lambda j, live: (j, 0, 0)),
            pl.BlockSpec((group, width, width), lambda j, live: (j, 0, 0)),
        ],
        out_specs=[
            pl.BlockSpec((fields, levels, group * width), lambda j, live: (0, 0, j)),
            pl.BlockSpec((group, fields, levels, width), lambda j, live: (j, 0, 0, 0)),
        ],
    )
    return pl.pallas_call(
        nest_kernel,
        grid_spec=grid_spec,
        out_shape=[jax.ShapeDtypeStruct(nest.shape, jnp.float32), jax.ShapeDtypeStruct(fetched.shape, jnp.float32)],
        compiler_params=pltpu.CompilerParams(vmem_limit_bytes=48 * 1024 * 1024),
    )(nest_live, nest_mixing, fetched, nest, relax.reshape(count, 1, width), nest_inverse, interp)


def body(
    parent,
    parent_inverse,
    nest,
    nest_inverse,
    interp,
    relax,
    src_list,
    nest_live,
    mixing,
    nest_mixing,
):
    fields, levels, parent_cols = parent.shape
    parent_count = parent_inverse.shape[0]
    nest_count = nest_inverse.shape[0]
    width = interp.shape[1]
    group = lax.axis_size("sub")

    padded = with_halo(parent, ((("tile", "sub"), 2),), 1)
    smoothed_all = parent + mixing[:, None, None] * (
        padded[:, :, :-2] + padded[:, :, 2:] - 2.0 * parent
    )

    owner = src_list // parent_count
    local = src_list % parent_count
    peers = jnp.arange(group, dtype=jnp.int32)
    named = owner[None, :] == peers[:, None]
    want = jnp.max(jnp.where(named, local[None, :], -1), axis=1)
    wanted = lax.all_to_all(want, "sub", split_axis=0, concat_axis=0, tiled=True)
    send_index = jnp.maximum(wanted, 0)
    gather_back = named.astype(jnp.float32)
    blocks = jnp.arange(parent_count, dtype=jnp.int32)
    place = (wanted[None, :] == blocks[:, None]).astype(jnp.float32)

    shaped = smoothed_all.reshape(fields, levels, parent_count, width)
    stepped = jnp.einsum("klm,fmkc->kflc", parent_inverse, shaped, precision=HIGH)
    outgoing = jnp.take(stepped, send_index, axis=0)
    arrived = lax.all_to_all(outgoing, "sub", split_axis=0, concat_axis=0, tiled=True)
    fetched = jnp.take(arrived, owner, axis=0)

    nest_out, change = nest_step(nest_live, nest_mixing, fetched, nest, relax, nest_inverse, interp)

    returning = jnp.einsum("oj,jflc->oflc", gather_back, change, precision=HIGH)
    landed = lax.all_to_all(returning, "sub", split_axis=0, concat_axis=0, tiled=True)
    summed = jnp.einsum("kg,gflc->kflc", place, landed, precision=HIGH)
    parent_out = stepped + FEEDBACK * summed
    parent_out = jnp.transpose(parent_out, (1, 2, 0, 3)).reshape(fields, levels, parent_cols)
    return parent_out, nest_out


def solution(mesh):
    cols = P(None, None, ("tile", "sub"))
    rows = P(("tile", "sub"), None, None)
    flat = P(("tile", "sub"))
    in_specs = (cols, rows, cols, rows, rows, flat, flat, flat, P(), P())
    out_specs = (cols, cols)
    return jax.shard_map(body, mesh=mesh, in_specs=in_specs, out_specs=out_specs, check_vma=False)
```

```python
import jax
import jax.numpy as jnp
from jax import lax
from jax.experimental import pallas as pl
from jax.experimental.pallas import tpu as pltpu
from jax.sharding import PartitionSpec as P

SUBSTEPS = 3


FEEDBACK = 0.25

HIGH = lax.Precision.HIGHEST


def with_halo(block, sides, width):
    for axis, dim in sides:
        count = lax.axis_size(axis)
        forward = [(i, i + 1) for i in range(count - 1)]
        forward.append((count - 1, 0))
        backward = [(target, source) for source, target in forward]
        low = lax.ppermute(
            lax.slice_in_dim(block, block.shape[dim] - width, None, axis=dim), axis, forward
        )
        high = lax.ppermute(lax.slice_in_dim(block, 0, width, axis=dim), axis, backward)
        block = jnp.concatenate([low, block, high], axis=dim)
    return block


def dot3(a, b, dims):
    ah = a.astype(jnp.bfloat16)
    al = (a - ah.astype(jnp.float32)).astype(jnp.bfloat16)
    bh = b.astype(jnp.bfloat16)
    bl = (b - bh.astype(jnp.float32)).astype(jnp.bfloat16)
    f = lambda x, y: lax.dot_general(x, y, dims, preferred_element_type=jnp.float32)
    return f(ah, bh) + (f(ah, bl) + f(al, bh))

ROWS = (((1,), (0,)), ((), ()))
COLS = (((1,), (1,)), ((), ()))

def nest_kernel(live_ref, coef_ref, fetched_ref, nest_ref, relax_ref, inv_ref, interp_ref, out_ref, change_ref):
    group, levels, fields, width = fetched_ref.shape
    lane = lax.broadcasted_iota(jnp.int32, (levels, fields * width), 1) % width
    coef = jnp.concatenate(
        [jnp.full((1, width), coef_ref[field], jnp.float32) for field in range(fields)], axis=1
    )
    for g in range(group):
        live = live_ref[pl.program_id(0) * group + g] == 1
        cols = slice(g * width, (g + 1) * width)
        weights = relax_ref[g]
        inverse = inv_ref[g]
        weights_ip = interp_ref[g]
        states = []
        forced = []
        for field in range(fields):
            state = nest_ref[:, field, cols]
            boundary = dot3(fetched_ref[g, :, field, :], weights_ip, COLS)
            states.append(state)
            forced.append(state + weights * (boundary - state))
        forced = jnp.concatenate(forced, axis=1)
        for substep in range(SUBSTEPS):
            lower = jnp.where(lane == 0, forced, pltpu.roll(forced, 1, 1))
            upper = jnp.where(lane == width - 1, forced, pltpu.roll(forced, fields * width - 1, 1))
            mixed = forced + coef * (lower + upper - 2.0 * forced)
            forced = dot3(inverse, mixed, ROWS)
        for field in range(fields):
            part = forced[:, field * width:(field + 1) * width]
            out_ref[:, field, cols] = jnp.where(live, part, states[field])
            restricted = dot3(part, weights_ip, ROWS)
            change_ref[g, :, field, :] = jnp.where(live, restricted - fetched_ref[g, :, field, :], 0.0)


def nest_step(nest_live, nest_mixing, fetched, nest, relax, nest_inverse, interp, group=4):
    count, levels, fields, width = fetched.shape
    grid_spec = pltpu.PrefetchScalarGridSpec(
        num_scalar_prefetch=1,
        grid=(count // group,),
        in_specs=[
            pl.BlockSpec(memory_space=pltpu.SMEM),
            pl.BlockSpec((group, levels, fields, width), lambda j, live: (j, 0, 0, 0)),
            pl.BlockSpec((levels, fields, group * width), lambda j, live: (0, 0, j)),
            pl.BlockSpec((group, 1, width), lambda j, live: (j, 0, 0)),
            pl.BlockSpec((group, levels, levels), lambda j, live: (j, 0, 0)),
            pl.BlockSpec((group, width, width), lambda j, live: (j, 0, 0)),
        ],
        out_specs=[
            pl.BlockSpec((levels, fields, group * width), lambda j, live: (0, 0, j)),
            pl.BlockSpec((group, levels, fields, width), lambda j, live: (j, 0, 0, 0)),
        ],
    )
    return pl.pallas_call(
        nest_kernel,
        grid_spec=grid_spec,
        out_shape=[jax.ShapeDtypeStruct(nest.shape, jnp.float32), jax.ShapeDtypeStruct(fetched.shape, jnp.float32)],
        compiler_params=pltpu.CompilerParams(vmem_limit_bytes=48 * 1024 * 1024),
    )(nest_live, nest_mixing, fetched, nest, relax.reshape(count, 1, width), nest_inverse, interp)


def body(
    parent,
    parent_inverse,
    nest,
    nest_inverse,
    interp,
    relax,
    src_list,
    nest_live,
    mixing,
    nest_mixing,
):
    fields, levels, parent_cols = parent.shape
    parent_count = parent_inverse.shape[0]
    nest_count = nest_inverse.shape[0]
    width = interp.shape[1]
    group = lax.axis_size("sub")

    parent_lf = jnp.transpose(parent, (1, 0, 2))
    padded = with_halo(parent_lf, ((("tile", "sub"), 2),), 1)
    smoothed = parent_lf + mixing[None, :, None] * (
        padded[:, :, :-2] + padded[:, :, 2:] - 2.0 * parent_lf
    )

    owner = src_list // parent_count
    local = src_list % parent_count
    peers = jnp.arange(group, dtype=jnp.int32)
    named = owner[None, :] == peers[:, None]
    want = jnp.max(jnp.where(named, local[None, :], -1), axis=1)
    wanted = lax.all_to_all(want, "sub", split_axis=0, concat_axis=0, tiled=True)
    send_index = jnp.maximum(wanted, 0)
    gather_back = named.astype(jnp.float32)
    blocks = jnp.arange(parent_count, dtype=jnp.int32)
    place = (wanted[None, :] == blocks[:, None]).astype(jnp.float32)

    shaped = smoothed.reshape(levels, fields, parent_count, width)
    stepped = jnp.einsum("klm,mfkc->klfc", parent_inverse, shaped, precision=HIGH)
    outgoing = jnp.take(stepped, send_index, axis=0, mode="clip")
    arrived = lax.all_to_all(outgoing, "sub", split_axis=0, concat_axis=0, tiled=True)
    fetched = jnp.take(arrived, owner, axis=0, mode="clip")

    nest_lf = jnp.transpose(nest, (1, 0, 2))
    nest_out, change = nest_step(nest_live, nest_mixing, fetched, nest_lf, relax, nest_inverse, interp)

    returning = jnp.einsum("oj,jlfc->olfc", gather_back, change, precision=HIGH)
    landed = lax.all_to_all(returning, "sub", split_axis=0, concat_axis=0, tiled=True)
    summed = jnp.einsum("kg,glfc->klfc", place, landed, precision=HIGH)
    parent_out = stepped + FEEDBACK * summed
    parent_out = jnp.transpose(parent_out, (2, 1, 0, 3)).reshape(fields, levels, parent_cols)
    return parent_out, jnp.transpose(nest_out, (1, 0, 2))


def solution(mesh):
    cols = P(None, None, ("tile", "sub"))
    rows = P(("tile", "sub"), None, None)
    flat = P(("tile", "sub"))
    in_specs = (cols, rows, cols, rows, rows, flat, flat, flat, P(), P())
    out_specs = (cols, cols)
    return jax.shard_map(body, mesh=mesh, in_specs=in_specs, out_specs=out_specs, check_vma=False)
```

```python
import jax
import jax.numpy as jnp
from jax import lax
from jax.experimental import pallas as pl
from jax.experimental.pallas import tpu as pltpu
from jax.sharding import Mesh
from jax.sharding import PartitionSpec as P

SUBSTEPS = 3


FEEDBACK = 0.25

HIGH = lax.Precision.HIGHEST


def with_halo(block, sides, width):
    for axis, dim in sides:
        count = lax.axis_size(axis)
        forward = [(i, i + 1) for i in range(count - 1)]
        forward.append((count - 1, 0))
        backward = [(target, source) for source, target in forward]
        low = lax.ppermute(
            lax.slice_in_dim(block, block.shape[dim] - width, None, axis=dim), axis, forward
        )
        high = lax.ppermute(lax.slice_in_dim(block, 0, width, axis=dim), axis, backward)
        block = jnp.concatenate([low, block, high], axis=dim)
    return block


def dot3(a, b, dims):
    ah = a.astype(jnp.bfloat16)
    al = (a - ah.astype(jnp.float32)).astype(jnp.bfloat16)
    bh = b.astype(jnp.bfloat16)
    bl = (b - bh.astype(jnp.float32)).astype(jnp.bfloat16)
    f = lambda x, y: lax.dot_general(x, y, dims, preferred_element_type=jnp.float32)
    return f(ah, bh) + (f(ah, bl) + f(al, bh))

ROWS = (((1,), (0,)), ((), ()))
COLS = (((1,), (1,)), ((), ()))

def nest_kernel(live_ref, coef_ref, fetched_ref, nest_ref, relax_ref, inv_ref, interp_ref, out_ref, change_ref):
    group, levels, fields, width = fetched_ref.shape
    lane = lax.broadcasted_iota(jnp.int32, (levels, fields * width), 1) % width
    coef = jnp.concatenate(
        [jnp.full((1, width), coef_ref[field], jnp.float32) for field in range(fields)], axis=1
    )
    for g in range(group):
        live = live_ref[pl.program_id(0) * group + g] == 1
        cols = slice(g * width, (g + 1) * width)
        weights = relax_ref[g]
        inverse = inv_ref[g]
        weights_ip = interp_ref[g]
        states = []
        forced = []
        for field in range(fields):
            state = nest_ref[:, field, cols]
            boundary = dot3(fetched_ref[g, :, field, :], weights_ip, COLS)
            states.append(state)
            forced.append(state + weights * (boundary - state))
        forced = jnp.concatenate(forced, axis=1)
        for substep in range(SUBSTEPS):
            lower = jnp.where(lane == 0, forced, pltpu.roll(forced, 1, 1))
            upper = jnp.where(lane == width - 1, forced, pltpu.roll(forced, fields * width - 1, 1))
            mixed = forced + coef * (lower + upper - 2.0 * forced)
            forced = dot3(inverse, mixed, ROWS)
        for field in range(fields):
            part = forced[:, field * width:(field + 1) * width]
            out_ref[:, field, cols] = jnp.where(live, part, states[field])
            restricted = dot3(part, weights_ip, ROWS)
            change_ref[g, :, field, :] = jnp.where(live, restricted - fetched_ref[g, :, field, :], 0.0)


def nest_step(nest_live, nest_mixing, fetched, nest, relax, nest_inverse, interp, group=4):
    count, levels, fields, width = fetched.shape
    grid_spec = pltpu.PrefetchScalarGridSpec(
        num_scalar_prefetch=1,
        grid=(count // group,),
        in_specs=[
            pl.BlockSpec(memory_space=pltpu.SMEM),
            pl.BlockSpec((group, levels, fields, width), lambda j, live: (j, 0, 0, 0)),
            pl.BlockSpec((levels, fields, group * width), lambda j, live: (0, 0, j)),
            pl.BlockSpec((group, 1, width), lambda j, live: (j, 0, 0)),
            pl.BlockSpec((group, levels, levels), lambda j, live: (j, 0, 0)),
            pl.BlockSpec((group, width, width), lambda j, live: (j, 0, 0)),
        ],
        out_specs=[
            pl.BlockSpec((levels, fields, group * width), lambda j, live: (0, 0, j)),
            pl.BlockSpec((group, levels, fields, width), lambda j, live: (j, 0, 0, 0)),
        ],
    )
    return pl.pallas_call(
        nest_kernel,
        grid_spec=grid_spec,
        out_shape=[jax.ShapeDtypeStruct(nest.shape, jnp.float32), jax.ShapeDtypeStruct(fetched.shape, jnp.float32)],
        compiler_params=pltpu.CompilerParams(vmem_limit_bytes=48 * 1024 * 1024),
    )(nest_live, nest_mixing, fetched, nest, relax.reshape(count, 1, width), nest_inverse, interp)


def body(
    parent,
    parent_inverse,
    nest,
    nest_inverse,
    interp,
    relax,
    src_list,
    nest_live,
    mixing,
    nest_mixing,
):
    fields, levels, parent_cols = parent.shape
    parent_count = parent_inverse.shape[0]
    nest_count = nest_inverse.shape[0]
    width = interp.shape[1]
    group = lax.axis_size(("z", "y"))

    parent_lf = jnp.transpose(parent, (1, 0, 2))
    padded = with_halo(parent_lf, ((("tile", "z", "y"), 2),), 1)
    smoothed = parent_lf + mixing[None, :, None] * (
        padded[:, :, :-2] + padded[:, :, 2:] - 2.0 * parent_lf
    )

    zs = lax.axis_size("z")
    ys = lax.axis_size("y")
    my_y = lax.axis_index("y")
    subs = ("z", "y")

    owner = src_list // parent_count
    local = src_list % parent_count
    peers = jnp.arange(group, dtype=jnp.int32)
    named = owner[None, :] == peers[:, None]
    want = jnp.max(jnp.where(named, local[None, :], -1), axis=1)
    wanted = lax.all_to_all(want, subs, split_axis=0, concat_axis=0, tiled=True)
    send_index = jnp.maximum(wanted, 0)
    gather_back = named.astype(jnp.float32)
    blocks = jnp.arange(parent_count, dtype=jnp.int32)
    place = (wanted[None, :] == blocks[:, None]).astype(jnp.float32)

    owner_z = owner // ys
    owner_y = owner % ys
    slot = owner_y * zs + owner_z
    row_lists = lax.all_gather(src_list, "y", axis=0, tiled=False)
    row_owner = row_lists // parent_count
    row_local = row_lists % parent_count
    column = jnp.arange(zs, dtype=jnp.int32) * ys + my_y
    hit = row_owner[:, :, None] == column[None, None, :]
    pick = jnp.max(jnp.where(hit, row_local[:, :, None], 0), axis=1)
    index = (jnp.arange(zs, dtype=jnp.int32)[None, :] * parent_count + pick).reshape(-1)
    slots = jnp.arange(ys * zs, dtype=jnp.int32)
    stage_back = (slot[None, :] == slots[:, None]).astype(jnp.float32)
    stage_place = pick[:, :, None] == blocks[None, None, :]

    shaped = smoothed.reshape(levels, fields, parent_count, width)
    stepped = jnp.einsum("klm,mfkc->klfc", parent_inverse, shaped, precision=HIGH)
    half = fields // 2
    direct, staged = stepped[:, :, :half], stepped[:, :, half:]

    outgoing = jnp.take(direct, send_index, axis=0, mode="clip")
    arrived = lax.all_to_all(outgoing, subs, split_axis=0, concat_axis=0, tiled=True)
    fetched_direct = jnp.take(arrived, owner, axis=0, mode="clip")
    gathered = lax.all_gather(staged, "z", axis=0, tiled=True)
    relayed = jnp.take(gathered, index, axis=0, mode="clip")
    reached = lax.all_to_all(relayed, "y", split_axis=0, concat_axis=0, tiled=True)
    fetched_staged = jnp.take(reached, slot, axis=0, mode="clip")
    fetched = jnp.concatenate([fetched_direct, fetched_staged], axis=2)

    nest_lf = jnp.transpose(nest, (1, 0, 2))
    nest_out, change = nest_step(nest_live, nest_mixing, fetched, nest_lf, relax, nest_inverse, interp)

    change_direct, change_staged = change[:, :, :half], change[:, :, half:]
    returning = jnp.einsum("oj,jlfc->olfc", gather_back, change_direct, precision=HIGH)
    landed = lax.all_to_all(returning, subs, split_axis=0, concat_axis=0, tiled=True)
    summed_direct = jnp.einsum("kg,glfc->klfc", place, landed, precision=HIGH)

    back = jnp.einsum("qj,jlfc->qlfc", stage_back, change_staged, precision=HIGH)
    back = lax.all_to_all(back, "y", split_axis=0, concat_axis=0, tiled=True)
    back = back.reshape((ys, zs) + back.shape[1:])
    partial = jnp.sum(jnp.where(stage_place[:, :, :, None, None, None], back[:, :, None], 0.0), axis=0)
    partial = partial.reshape((zs * parent_count,) + partial.shape[2:])
    summed_staged = lax.psum_scatter(partial, "z", scatter_dimension=0, tiled=True)

    summed = jnp.concatenate([summed_direct, summed_staged], axis=2)
    parent_out = stepped + FEEDBACK * summed
    parent_out = jnp.transpose(parent_out, (2, 1, 0, 3)).reshape(fields, levels, parent_cols)
    return parent_out, jnp.transpose(nest_out, (1, 0, 2))


def split_mesh(mesh):
    devices = mesh.devices
    tiles, subs = devices.shape
    try:
        ys = len({d.coords[1] for d in devices[0]})
    except Exception:
        ys = 4
    if subs % ys:
        ys = 1
    return Mesh(devices.reshape(tiles, subs // ys, ys), ("tile", "z", "y"))


def solution(mesh):
    inner = split_mesh(mesh)
    cols = P(None, None, ("tile", "z", "y"))
    rows = P(("tile", "z", "y"), None, None)
    flat = P(("tile", "z", "y"))
    in_specs = (cols, rows, cols, rows, rows, flat, flat, flat, P(), P())
    out_specs = (cols, cols)
    return jax.shard_map(body, mesh=inner, in_specs=in_specs, out_specs=out_specs, check_vma=False)
```

```python
import jax
import jax.numpy as jnp
from jax import lax
from jax.experimental import pallas as pl
from jax.experimental.pallas import tpu as pltpu
from jax.sharding import PartitionSpec as P

SUBSTEPS = 3


FEEDBACK = 0.25

HIGH = lax.Precision.HIGHEST


def with_halo(block, sides, width):
    for axis, dim in sides:
        count = lax.axis_size(axis)
        forward = [(i, i + 1) for i in range(count - 1)]
        forward.append((count - 1, 0))
        backward = [(target, source) for source, target in forward]
        low = lax.ppermute(
            lax.slice_in_dim(block, block.shape[dim] - width, None, axis=dim), axis, forward
        )
        high = lax.ppermute(lax.slice_in_dim(block, 0, width, axis=dim), axis, backward)
        block = jnp.concatenate([low, block, high], axis=dim)
    return block


def dot3(a, b, dims):
    ah = a.astype(jnp.bfloat16)
    al = (a - ah.astype(jnp.float32)).astype(jnp.bfloat16)
    bh = b.astype(jnp.bfloat16)
    bl = (b - bh.astype(jnp.float32)).astype(jnp.bfloat16)
    f = lambda x, y: lax.dot_general(x, y, dims, preferred_element_type=jnp.float32)
    return f(ah, bh) + (f(ah, bl) + f(al, bh))

ROWS = (((1,), (0,)), ((), ()))
COLS = (((1,), (1,)), ((), ()))

def nest_kernel(live_ref, coef_ref, fetched_ref, nest_ref, relax_ref, inv_ref, interp_ref, out_ref, change_ref):
    group, levels, fields, width = fetched_ref.shape
    lane = lax.broadcasted_iota(jnp.int32, (levels, fields * width), 1) % width
    coef = jnp.concatenate(
        [jnp.full((1, width), coef_ref[field], jnp.float32) for field in range(fields)], axis=1
    )
    for g in range(group):
        live = live_ref[pl.program_id(0) * group + g] == 1
        cols = slice(g * width, (g + 1) * width)
        weights = relax_ref[g]
        inverse = inv_ref[g]
        weights_ip = interp_ref[g]
        states = []
        forced = []
        for field in range(fields):
            state = nest_ref[:, field, cols]
            boundary = dot3(fetched_ref[g, :, field, :], weights_ip, COLS)
            states.append(state)
            forced.append(state + weights * (boundary - state))
        forced = jnp.concatenate(forced, axis=1)
        for substep in range(SUBSTEPS):
            lower = jnp.where(lane == 0, forced, pltpu.roll(forced, 1, 1))
            upper = jnp.where(lane == width - 1, forced, pltpu.roll(forced, fields * width - 1, 1))
            mixed = forced + coef * (lower + upper - 2.0 * forced)
            forced = dot3(inverse, mixed, ROWS)
        for field in range(fields):
            part = forced[:, field * width:(field + 1) * width]
            out_ref[:, field, cols] = jnp.where(live, part, states[field])
            restricted = dot3(part, weights_ip, ROWS)
            change_ref[g, :, field, :] = jnp.where(live, restricted - fetched_ref[g, :, field, :], 0.0)


def nest_step(nest_live, nest_mixing, fetched, nest, relax, nest_inverse, interp, group=4):
    count, levels, fields, width = fetched.shape
    grid_spec = pltpu.PrefetchScalarGridSpec(
        num_scalar_prefetch=1,
        grid=(count // group,),
        in_specs=[
            pl.BlockSpec(memory_space=pltpu.SMEM),
            pl.BlockSpec((group, levels, fields, width), lambda j, live: (j, 0, 0, 0)),
            pl.BlockSpec((levels, fields, group * width), lambda j, live: (0, 0, j)),
            pl.BlockSpec((group, 1, width), lambda j, live: (j, 0, 0)),
            pl.BlockSpec((group, levels, levels), lambda j, live: (j, 0, 0)),
            pl.BlockSpec((group, width, width), lambda j, live: (j, 0, 0)),
        ],
        out_specs=[
            pl.BlockSpec((levels, fields, group * width), lambda j, live: (0, 0, j)),
            pl.BlockSpec((group, levels, fields, width), lambda j, live: (j, 0, 0, 0)),
        ],
    )
    return pl.pallas_call(
        nest_kernel,
        grid_spec=grid_spec,
        out_shape=[jax.ShapeDtypeStruct(nest.shape, jnp.float32), jax.ShapeDtypeStruct(fetched.shape, jnp.float32)],
        compiler_params=pltpu.CompilerParams(vmem_limit_bytes=48 * 1024 * 1024),
    )(nest_live, nest_mixing, fetched, nest, relax.reshape(count, 1, width), nest_inverse, interp)


def body(
    parent,
    parent_inverse,
    nest,
    nest_inverse,
    interp,
    relax,
    src_list,
    nest_live,
    mixing,
    nest_mixing,
):
    fields, levels, parent_cols = parent.shape
    parent_count = parent_inverse.shape[0]
    nest_count = nest_inverse.shape[0]
    width = interp.shape[1]
    group = lax.axis_size("sub")

    parent_lf = jnp.transpose(parent, (1, 0, 2))
    padded = with_halo(parent_lf, ((("tile", "sub"), 2),), 1)
    smoothed = parent_lf + mixing[None, :, None] * (
        padded[:, :, :-2] + padded[:, :, 2:] - 2.0 * parent_lf
    )

    owner = src_list // parent_count
    local = src_list % parent_count
    peers = jnp.arange(group, dtype=jnp.int32)
    named = owner[None, :] == peers[:, None]
    want = jnp.max(jnp.where(named, local[None, :], -1), axis=1)
    wanted = lax.all_to_all(want, "sub", split_axis=0, concat_axis=0, tiled=True)
    send_index = jnp.maximum(wanted, 0)
    gather_back = named.astype(jnp.float32)
    blocks = jnp.arange(parent_count, dtype=jnp.int32)
    place = (wanted[None, :] == blocks[:, None]).astype(jnp.float32)

    shaped = smoothed.reshape(levels, fields, parent_count, width)
    stepped = jnp.einsum("klm,mfkc->klfc", parent_inverse, shaped, precision=HIGH)
    outgoing = sum(
        jnp.where((send_index == k)[:, None, None, None], stepped[k][None], 0.0)
        for k in range(parent_count)
    )
    arrived = lax.all_to_all(outgoing, "sub", split_axis=0, concat_axis=0, tiled=True)
    fetched = jnp.take(arrived, owner, axis=0, mode="clip")

    nest_lf = jnp.transpose(nest, (1, 0, 2))
    nest_out, change = nest_step(nest_live, nest_mixing, fetched, nest_lf, relax, nest_inverse, interp)

    returning = jnp.einsum("oj,jlfc->olfc", gather_back, change, precision=HIGH)
    landed = lax.all_to_all(returning, "sub", split_axis=0, concat_axis=0, tiled=True)
    summed = jnp.einsum("kg,glfc->klfc", place, landed, precision=HIGH)
    parent_out = stepped + FEEDBACK * summed
    parent_out = jnp.transpose(parent_out, (2, 1, 0, 3)).reshape(fields, levels, parent_cols)
    return parent_out, jnp.transpose(nest_out, (1, 0, 2))


def solution(mesh):
    cols = P(None, None, ("tile", "sub"))
    rows = P(("tile", "sub"), None, None)
    flat = P(("tile", "sub"))
    in_specs = (cols, rows, cols, rows, rows, flat, flat, flat, P(), P())
    out_specs = (cols, cols)
    return jax.shard_map(body, mesh=mesh, in_specs=in_specs, out_specs=out_specs, check_vma=False)
```

```python
import functools

import jax
import jax.numpy as jnp
from jax import lax
from jax.experimental import pallas as pl
from jax.experimental.pallas import tpu as pltpu
from jax.sharding import PartitionSpec as P

SUBSTEPS = 3


FEEDBACK = 0.25

HIGH = lax.Precision.HIGHEST


def with_halo(block, sides, width):
    for axis, dim in sides:
        count = lax.axis_size(axis)
        forward = [(i, i + 1) for i in range(count - 1)]
        forward.append((count - 1, 0))
        backward = [(target, source) for source, target in forward]
        low = lax.ppermute(
            lax.slice_in_dim(block, block.shape[dim] - width, None, axis=dim), axis, forward
        )
        high = lax.ppermute(lax.slice_in_dim(block, 0, width, axis=dim), axis, backward)
        block = jnp.concatenate([low, block, high], axis=dim)
    return block


def dot3(a, b, dims):
    ah = a.astype(jnp.bfloat16)
    al = (a - ah.astype(jnp.float32)).astype(jnp.bfloat16)
    bh = b.astype(jnp.bfloat16)
    bl = (b - bh.astype(jnp.float32)).astype(jnp.bfloat16)
    f = lambda x, y: lax.dot_general(x, y, dims, preferred_element_type=jnp.float32)
    return f(ah, bh) + (f(ah, bl) + f(al, bh))

ROWS = (((1,), (0,)), ((), ()))
COLS = (((1,), (1,)), ((), ()))

def nest_kernel(which, live_ref, coef_ref, fetched_ref, nest_ref, relax_ref, inv_ref, interp_ref, out_ref):
    group, levels, fields, width = fetched_ref.shape
    lane = lax.broadcasted_iota(jnp.int32, (levels, fields * width), 1) % width
    coef = jnp.concatenate(
        [jnp.full((1, width), coef_ref[field], jnp.float32) for field in range(fields)], axis=1
    )
    for g in range(group):
        live = live_ref[pl.program_id(0) * group + g] == 1
        cols = slice(g * width, (g + 1) * width)
        weights = relax_ref[g]
        inverse = inv_ref[g]
        weights_ip = interp_ref[g]
        states = []
        forced = []
        for field in range(fields):
            state = nest_ref[:, field, cols]
            boundary = dot3(fetched_ref[g, :, field, :], weights_ip, COLS)
            states.append(state)
            forced.append(state + weights * (boundary - state))
        forced = jnp.concatenate(forced, axis=1)
        for substep in range(SUBSTEPS):
            lower = jnp.where(lane == 0, forced, pltpu.roll(forced, 1, 1))
            upper = jnp.where(lane == width - 1, forced, pltpu.roll(forced, fields * width - 1, 1))
            mixed = forced + coef * (lower + upper - 2.0 * forced)
            forced = dot3(inverse, mixed, ROWS)
        for field in range(fields):
            part = forced[:, field * width:(field + 1) * width]
            if which == "state":
                out_ref[:, field, cols] = jnp.where(live, part, states[field])
            else:
                restricted = dot3(part, weights_ip, ROWS)
                out_ref[g, :, field, :] = jnp.where(live, restricted - fetched_ref[g, :, field, :], 0.0)


def nest_step(which, nest_live, nest_mixing, fetched, nest, relax, nest_inverse, interp, group=4):
    count, levels, fields, width = fetched.shape
    if which == "state":
        out_spec = pl.BlockSpec((levels, fields, group * width), lambda j, live: (0, 0, j))
        out_shape = jax.ShapeDtypeStruct(nest.shape, jnp.float32)
    else:
        out_spec = pl.BlockSpec((group, levels, fields, width), lambda j, live: (j, 0, 0, 0))
        out_shape = jax.ShapeDtypeStruct(fetched.shape, jnp.float32)
    grid_spec = pltpu.PrefetchScalarGridSpec(
        num_scalar_prefetch=1,
        grid=(count // group,),
        in_specs=[
            pl.BlockSpec(memory_space=pltpu.SMEM),
            pl.BlockSpec((group, levels, fields, width), lambda j, live: (j, 0, 0, 0)),
            pl.BlockSpec((levels, fields, group * width), lambda j, live: (0, 0, j)),
            pl.BlockSpec((group, 1, width), lambda j, live: (j, 0, 0)),
            pl.BlockSpec((group, levels, levels), lambda j, live: (j, 0, 0)),
            pl.BlockSpec((group, width, width), lambda j, live: (j, 0, 0)),
        ],
        out_specs=out_spec,
    )
    block_bytes = 4 * count * levels * fields * width
    flops = 6 * count * fields * levels * width * (2 * width + SUBSTEPS * levels)
    return pl.pallas_call(
        functools.partial(nest_kernel, which),
        grid_spec=grid_spec,
        out_shape=out_shape,
        compiler_params=pltpu.CompilerParams(vmem_limit_bytes=48 * 1024 * 1024),
        cost_estimate=pl.CostEstimate(flops=flops, bytes_accessed=3 * block_bytes, transcendentals=0),
    )(nest_live, nest_mixing, fetched, nest, relax.reshape(count, 1, width), nest_inverse, interp)


def body(
    parent,
    parent_inverse,
    nest,
    nest_inverse,
    interp,
    relax,
    src_list,
    nest_live,
    mixing,
    nest_mixing,
):
    fields, levels, parent_cols = parent.shape
    parent_count = parent_inverse.shape[0]
    nest_count = nest_inverse.shape[0]
    width = interp.shape[1]
    group = lax.axis_size("sub")

    parent_lf = jnp.transpose(parent, (1, 0, 2))
    padded = with_halo(parent_lf, ((("tile", "sub"), 2),), 1)
    smoothed = parent_lf + mixing[None, :, None] * (
        padded[:, :, :-2] + padded[:, :, 2:] - 2.0 * parent_lf
    )

    owner = src_list // parent_count
    local = src_list % parent_count
    peers = jnp.arange(group, dtype=jnp.int32)
    named = owner[None, :] == peers[:, None]
    want = jnp.max(jnp.where(named, local[None, :], -1), axis=1)
    wanted = lax.all_to_all(want, "sub", split_axis=0, concat_axis=0, tiled=True)
    send_index = jnp.maximum(wanted, 0)
    gather_back = named.astype(jnp.float32)
    blocks = jnp.arange(parent_count, dtype=jnp.int32)
    place = (wanted[None, :] == blocks[:, None]).astype(jnp.float32)

    shaped = smoothed.reshape(levels, fields, parent_count, width)
    stepped = jnp.einsum("klm,mfkc->klfc", parent_inverse, shaped, precision=HIGH)
    outgoing = sum(
        jnp.where((send_index == k)[:, None, None, None], stepped[k][None], 0.0)
        for k in range(parent_count)
    )
    arrived = lax.all_to_all(outgoing, "sub", split_axis=0, concat_axis=0, tiled=True)
    fetched = jnp.take(arrived, owner, axis=0, mode="clip")

    nest_lf = jnp.transpose(nest, (1, 0, 2))
    change = nest_step("change", nest_live, nest_mixing, fetched, nest_lf, relax, nest_inverse, interp)
    nest_out = nest_step("state", nest_live, nest_mixing, fetched, nest_lf, relax, nest_inverse, interp)

    returning = jnp.einsum("oj,jlfc->olfc", gather_back, change, precision=HIGH)
    landed = lax.all_to_all(returning, "sub", split_axis=0, concat_axis=0, tiled=True)
    summed = jnp.einsum("kg,glfc->klfc", place, landed, precision=HIGH)
    parent_out = stepped + FEEDBACK * summed
    parent_out = jnp.transpose(parent_out, (2, 1, 0, 3)).reshape(fields, levels, parent_cols)
    return parent_out, jnp.transpose(nest_out, (1, 0, 2))


def solution(mesh):
    cols = P(None, None, ("tile", "sub"))
    rows = P(("tile", "sub"), None, None)
    flat = P(("tile", "sub"))
    in_specs = (cols, rows, cols, rows, rows, flat, flat, flat, P(), P())
    out_specs = (cols, cols)
    return jax.shard_map(body, mesh=mesh, in_specs=in_specs, out_specs=out_specs, check_vma=False)
```

```python
import jax
import jax.numpy as jnp
from jax import lax
from jax.experimental import pallas as pl
from jax.experimental.pallas import tpu as pltpu
from jax.sharding import PartitionSpec as P

SUBSTEPS = 3


FEEDBACK = 0.25

HIGH = lax.Precision.HIGHEST


def with_halo(block, sides, width):
    for axis, dim in sides:
        count = lax.axis_size(axis)
        forward = [(i, i + 1) for i in range(count - 1)]
        forward.append((count - 1, 0))
        backward = [(target, source) for source, target in forward]
        low = lax.ppermute(
            lax.slice_in_dim(block, block.shape[dim] - width, None, axis=dim), axis, forward
        )
        high = lax.ppermute(lax.slice_in_dim(block, 0, width, axis=dim), axis, backward)
        block = jnp.concatenate([low, block, high], axis=dim)
    return block


def dot3(a, b, dims):
    ah = a.astype(jnp.bfloat16)
    al = (a - ah.astype(jnp.float32)).astype(jnp.bfloat16)
    bh = b.astype(jnp.bfloat16)
    bl = (b - bh.astype(jnp.float32)).astype(jnp.bfloat16)
    f = lambda x, y: lax.dot_general(x, y, dims, preferred_element_type=jnp.float32)
    return f(ah, bh) + (f(ah, bl) + f(al, bh))

ROWS = (((1,), (0,)), ((), ()))
COLS = (((1,), (1,)), ((), ()))

def nest_kernel(live_ref, coef_ref, fetched_ref, nest_ref, relax_ref, inv_ref, interp_ref, out_ref, change_ref, rows_ref):
    levels, fields, span = nest_ref.shape
    group = fetched_ref.shape[0]
    width = span // group
    lane = lax.broadcasted_iota(jnp.int32, (levels, fields * width), 1) % width
    coef = jnp.concatenate(
        [jnp.full((1, width), coef_ref[field], jnp.float32) for field in range(fields)], axis=1
    )
    for g in range(group):
        live = live_ref[pl.program_id(0) * group + g] == 1
        cols = slice(g * width, (g + 1) * width)
        weights = relax_ref[g]
        inverse = inv_ref[g]
        weights_ip = interp_ref[g]
        rows_ref[...] = dot3(fetched_ref[g], weights_ip, COLS)
        states = []
        forced = []
        for field in range(fields):
            state = nest_ref[:, field, cols]
            boundary = rows_ref[pl.ds(field, levels, stride=fields), :]
            states.append(state)
            forced.append(state + weights * (boundary - state))
        forced = jnp.concatenate(forced, axis=1)
        for substep in range(SUBSTEPS):
            lower = jnp.where(lane == 0, forced, pltpu.roll(forced, 1, 1))
            upper = jnp.where(lane == width - 1, forced, pltpu.roll(forced, fields * width - 1, 1))
            mixed = forced + coef * (lower + upper - 2.0 * forced)
            forced = dot3(inverse, mixed, ROWS)
        for field in range(fields):
            part = forced[:, field * width:(field + 1) * width]
            out_ref[:, field, cols] = jnp.where(live, part, states[field])
            rows_ref[pl.ds(field, levels, stride=fields), :] = part
        restricted = dot3(rows_ref[...], weights_ip, ROWS)
        change_ref[g] = jnp.where(live, restricted - fetched_ref[g], 0.0)


def nest_step(nest_live, nest_mixing, fetched, nest, relax, nest_inverse, interp, group=4):
    count, pairs, width = fetched.shape
    levels, fields, _ = nest.shape
    grid_spec = pltpu.PrefetchScalarGridSpec(
        num_scalar_prefetch=1,
        grid=(count // group,),
        in_specs=[
            pl.BlockSpec(memory_space=pltpu.SMEM),
            pl.BlockSpec((group, pairs, width), lambda j, live: (j, 0, 0)),
            pl.BlockSpec((levels, fields, group * width), lambda j, live: (0, 0, j)),
            pl.BlockSpec((group, 1, width), lambda j, live: (j, 0, 0)),
            pl.BlockSpec((group, levels, levels), lambda j, live: (j, 0, 0)),
            pl.BlockSpec((group, width, width), lambda j, live: (j, 0, 0)),
        ],
        out_specs=[
            pl.BlockSpec((levels, fields, group * width), lambda j, live: (0, 0, j)),
            pl.BlockSpec((group, pairs, width), lambda j, live: (j, 0, 0)),
        ],
        scratch_shapes=[pltpu.VMEM((pairs, width), jnp.float32)],
    )
    return pl.pallas_call(
        nest_kernel,
        grid_spec=grid_spec,
        out_shape=[jax.ShapeDtypeStruct(nest.shape, jnp.float32), jax.ShapeDtypeStruct(fetched.shape, jnp.float32)],
        compiler_params=pltpu.CompilerParams(vmem_limit_bytes=48 * 1024 * 1024),
    )(nest_live, nest_mixing, fetched, nest, relax.reshape(count, 1, width), nest_inverse, interp)


def body(
    parent,
    parent_inverse,
    nest,
    nest_inverse,
    interp,
    relax,
    src_list,
    nest_live,
    mixing,
    nest_mixing,
):
    fields, levels, parent_cols = parent.shape
    parent_count = parent_inverse.shape[0]
    nest_count = nest_inverse.shape[0]
    width = interp.shape[1]
    group = lax.axis_size("sub")

    parent_lf = jnp.transpose(parent, (1, 0, 2))
    padded = with_halo(parent_lf, ((("tile", "sub"), 2),), 1)
    smoothed = parent_lf + mixing[None, :, None] * (
        padded[:, :, :-2] + padded[:, :, 2:] - 2.0 * parent_lf
    )

    owner = src_list // parent_count
    local = src_list % parent_count
    peers = jnp.arange(group, dtype=jnp.int32)
    named = owner[None, :] == peers[:, None]
    want = jnp.max(jnp.where(named, local[None, :], -1), axis=1)
    wanted = lax.all_to_all(want, "sub", split_axis=0, concat_axis=0, tiled=True)
    send_index = jnp.maximum(wanted, 0)
    gather_back = named.astype(jnp.float32)
    blocks = jnp.arange(parent_count, dtype=jnp.int32)
    place = (wanted[None, :] == blocks[:, None]).astype(jnp.float32)

    shaped = smoothed.reshape(levels, fields, parent_count, width)
    stepped = jnp.einsum("klm,mfkc->klfc", parent_inverse, shaped, precision=HIGH)
    outgoing = sum(
        jnp.where((send_index == k)[:, None, None, None], stepped[k][None], 0.0)
        for k in range(parent_count)
    )
    arrived = lax.all_to_all(outgoing, "sub", split_axis=0, concat_axis=0, tiled=True)
    fetched = jnp.take(arrived, owner, axis=0, mode="clip")
    fetched = fetched.reshape(nest_count, levels * fields, width)

    nest_lf = jnp.transpose(nest, (1, 0, 2))
    nest_out, change = nest_step(nest_live, nest_mixing, fetched, nest_lf, relax, nest_inverse, interp)

    returning = jnp.einsum("oj,jrc->orc", gather_back, change, precision=HIGH)
    returning = returning.reshape(group, levels, fields, width)
    landed = lax.all_to_all(returning, "sub", split_axis=0, concat_axis=0, tiled=True)
    summed = jnp.einsum("kg,glfc->klfc", place, landed, precision=HIGH)
    parent_out = stepped + FEEDBACK * summed
    parent_out = jnp.transpose(parent_out, (2, 1, 0, 3)).reshape(fields, levels, parent_cols)
    return parent_out, jnp.transpose(nest_out, (1, 0, 2))


def solution(mesh):
    cols = P(None, None, ("tile", "sub"))
    rows = P(("tile", "sub"), None, None)
    flat = P(("tile", "sub"))
    in_specs = (cols, rows, cols, rows, rows, flat, flat, flat, P(), P())
    out_specs = (cols, cols)
    return jax.shard_map(body, mesh=mesh, in_specs=in_specs, out_specs=out_specs, check_vma=False)
```

```python
import jax
import jax.numpy as jnp
from jax import lax
from jax.experimental import pallas as pl
from jax.experimental.pallas import tpu as pltpu
from jax.sharding import PartitionSpec as P

SUBSTEPS = 3


FEEDBACK = 0.25

HIGH = lax.Precision.HIGHEST


def with_halo(block, sides, width):
    for axis, dim in sides:
        count = lax.axis_size(axis)
        forward = [(i, i + 1) for i in range(count - 1)]
        forward.append((count - 1, 0))
        backward = [(target, source) for source, target in forward]
        low = lax.ppermute(
            lax.slice_in_dim(block, block.shape[dim] - width, None, axis=dim), axis, forward
        )
        high = lax.ppermute(lax.slice_in_dim(block, 0, width, axis=dim), axis, backward)
        block = jnp.concatenate([low, block, high], axis=dim)
    return block


def dot3(a, b, dims):
    ah = a.astype(jnp.bfloat16)
    al = (a - ah.astype(jnp.float32)).astype(jnp.bfloat16)
    bh = b.astype(jnp.bfloat16)
    bl = (b - bh.astype(jnp.float32)).astype(jnp.bfloat16)
    f = lambda x, y: lax.dot_general(x, y, dims, preferred_element_type=jnp.float32)
    return f(ah, bh) + (f(ah, bl) + f(al, bh))

ROWS = (((1,), (0,)), ((), ()))
COLS = (((1,), (1,)), ((), ()))

def nest_kernel(live_ref, owner_ref, coef_ref, *refs):
    *fetched_refs, nest_ref, relax_ref, inv_ref, interp_ref, out_ref, change_ref = refs
    group = len(fetched_refs)
    _, levels, fields, width = fetched_refs[0].shape
    lane = lax.broadcasted_iota(jnp.int32, (levels, fields * width), 1) % width
    coef = jnp.concatenate(
        [jnp.full((1, width), coef_ref[field], jnp.float32) for field in range(fields)], axis=1
    )
    for g in range(group):
        live = live_ref[pl.program_id(0) * group + g] == 1
        cols = slice(g * width, (g + 1) * width)
        weights = relax_ref[g]
        inverse = inv_ref[g]
        weights_ip = interp_ref[g]
        states = []
        forced = []
        for field in range(fields):
            state = nest_ref[:, field, cols]
            boundary = dot3(fetched_refs[g][0, :, field, :], weights_ip, COLS)
            states.append(state)
            forced.append(state + weights * (boundary - state))
        forced = jnp.concatenate(forced, axis=1)
        for substep in range(SUBSTEPS):
            lower = jnp.where(lane == 0, forced, pltpu.roll(forced, 1, 1))
            upper = jnp.where(lane == width - 1, forced, pltpu.roll(forced, fields * width - 1, 1))
            mixed = forced + coef * (lower + upper - 2.0 * forced)
            forced = dot3(inverse, mixed, ROWS)
        for field in range(fields):
            part = forced[:, field * width:(field + 1) * width]
            out_ref[:, field, cols] = jnp.where(live, part, states[field])
            restricted = dot3(part, weights_ip, ROWS)
            change_ref[g, :, field, :] = jnp.where(live, restricted - fetched_refs[g][0, :, field, :], 0.0)


def nest_step(nest_live, owner, nest_mixing, arrived, nest, relax, nest_inverse, interp, group=4):
    levels, fields, span = nest.shape
    width = interp.shape[1]
    count = span // width

    def named(g):
        return pl.BlockSpec(
            (1, levels, fields, width), lambda j, live, src: (src[j * group + g], 0, 0, 0)
        )

    grid_spec = pltpu.PrefetchScalarGridSpec(
        num_scalar_prefetch=2,
        grid=(count // group,),
        in_specs=[pl.BlockSpec(memory_space=pltpu.SMEM)]
        + [named(g) for g in range(group)]
        + [
            pl.BlockSpec((levels, fields, group * width), lambda j, live, src: (0, 0, j)),
            pl.BlockSpec((group, 1, width), lambda j, live, src: (j, 0, 0)),
            pl.BlockSpec((group, levels, levels), lambda j, live, src: (j, 0, 0)),
            pl.BlockSpec((group, width, width), lambda j, live, src: (j, 0, 0)),
        ],
        out_specs=[
            pl.BlockSpec((levels, fields, group * width), lambda j, live, src: (0, 0, j)),
            pl.BlockSpec((group, levels, fields, width), lambda j, live, src: (j, 0, 0, 0)),
        ],
    )
    return pl.pallas_call(
        nest_kernel,
        grid_spec=grid_spec,
        out_shape=[
            jax.ShapeDtypeStruct(nest.shape, jnp.float32),
            jax.ShapeDtypeStruct((count, levels, fields, width), jnp.float32),
        ],
        compiler_params=pltpu.CompilerParams(vmem_limit_bytes=48 * 1024 * 1024),
    )(nest_live, owner, nest_mixing, *([arrived] * group), nest, relax.reshape(count, 1, width), nest_inverse, interp)


def body(
    parent,
    parent_inverse,
    nest,
    nest_inverse,
    interp,
    relax,
    src_list,
    nest_live,
    mixing,
    nest_mixing,
):
    fields, levels, parent_cols = parent.shape
    parent_count = parent_inverse.shape[0]
    nest_count = nest_inverse.shape[0]
    width = interp.shape[1]
    group = lax.axis_size("sub")

    parent_lf = jnp.transpose(parent, (1, 0, 2))
    padded = with_halo(parent_lf, ((("tile", "sub"), 2),), 1)
    smoothed = parent_lf + mixing[None, :, None] * (
        padded[:, :, :-2] + padded[:, :, 2:] - 2.0 * parent_lf
    )

    owner = src_list // parent_count
    local = src_list % parent_count
    peers = jnp.arange(group, dtype=jnp.int32)
    named = owner[None, :] == peers[:, None]
    want = jnp.max(jnp.where(named, local[None, :], -1), axis=1)
    wanted = lax.all_to_all(want, "sub", split_axis=0, concat_axis=0, tiled=True)
    send_index = jnp.maximum(wanted, 0)
    gather_back = named.astype(jnp.float32)
    blocks = jnp.arange(parent_count, dtype=jnp.int32)
    place = (wanted[None, :] == blocks[:, None]).astype(jnp.float32)

    shaped = smoothed.reshape(levels, fields, parent_count, width)
    stepped = jnp.einsum("klm,mfkc->klfc", parent_inverse, shaped, precision=HIGH)
    outgoing = sum(
        jnp.where((send_index == k)[:, None, None, None], stepped[k][None], 0.0)
        for k in range(parent_count)
    )
    arrived = lax.all_to_all(outgoing, "sub", split_axis=0, concat_axis=0, tiled=True)

    nest_lf = jnp.transpose(nest, (1, 0, 2))
    nest_out, change = nest_step(nest_live, owner, nest_mixing, arrived, nest_lf, relax, nest_inverse, interp)

    returning = jnp.einsum("oj,jlfc->olfc", gather_back, change, precision=HIGH)
    landed = lax.all_to_all(returning, "sub", split_axis=0, concat_axis=0, tiled=True)
    summed = jnp.einsum("kg,glfc->klfc", place, landed, precision=HIGH)
    parent_out = stepped + FEEDBACK * summed
    parent_out = jnp.transpose(parent_out, (2, 1, 0, 3)).reshape(fields, levels, parent_cols)
    return parent_out, jnp.transpose(nest_out, (1, 0, 2))


def solution(mesh):
    cols = P(None, None, ("tile", "sub"))
    rows = P(("tile", "sub"), None, None)
    flat = P(("tile", "sub"))
    in_specs = (cols, rows, cols, rows, rows, flat, flat, flat, P(), P())
    out_specs = (cols, cols)
    return jax.shard_map(body, mesh=mesh, in_specs=in_specs, out_specs=out_specs, check_vma=False)
```

```python
import jax
import jax.numpy as jnp
from jax import lax
from jax.experimental import pallas as pl
from jax.experimental.pallas import tpu as pltpu
from jax.sharding import PartitionSpec as P

SUBSTEPS = 3


FEEDBACK = 0.25

HIGH = lax.Precision.HIGHEST


def with_halo(block, sides, width):
    for axis, dim in sides:
        count = lax.axis_size(axis)
        forward = [(i, i + 1) for i in range(count - 1)]
        forward.append((count - 1, 0))
        backward = [(target, source) for source, target in forward]
        low = lax.ppermute(
            lax.slice_in_dim(block, block.shape[dim] - width, None, axis=dim), axis, forward
        )
        high = lax.ppermute(lax.slice_in_dim(block, 0, width, axis=dim), axis, backward)
        block = jnp.concatenate([low, block, high], axis=dim)
    return block


def dot3(a, b, dims):
    ah = a.astype(jnp.bfloat16)
    al = (a - ah.astype(jnp.float32)).astype(jnp.bfloat16)
    bh = b.astype(jnp.bfloat16)
    bl = (b - bh.astype(jnp.float32)).astype(jnp.bfloat16)
    f = lambda x, y: lax.dot_general(x, y, dims, preferred_element_type=jnp.float32)
    return f(ah, bh) + (f(ah, bl) + f(al, bh))

ROWS = (((1,), (0,)), ((), ()))
COLS = (((1,), (1,)), ((), ()))

def nest_kernel(live_ref, owner_ref, coef_ref, *refs):
    *fetched_refs, nest_ref, relax_ref, inv_ref, interp_ref, out_ref, change_ref = refs
    group = len(fetched_refs)
    _, levels, fields, width = fetched_refs[0].shape
    lane = lax.broadcasted_iota(jnp.int32, (levels, fields * width), 1) % width
    coef = jnp.concatenate(
        [jnp.full((1, width), coef_ref[field], jnp.float32) for field in range(fields)], axis=1
    )
    for g in range(group):
        live = live_ref[pl.program_id(0) * group + g] == 1
        cols = slice(g * width, (g + 1) * width)
        weights = relax_ref[g]
        inverse = inv_ref[g]
        weights_ip = interp_ref[g]
        states = []
        forced = []
        for field in range(fields):
            state = nest_ref[:, field, cols]
            boundary = dot3(fetched_refs[g][0, :, field, :], weights_ip, COLS)
            states.append(state)
            forced.append(state + weights * (boundary - state))
        forced = jnp.concatenate(forced, axis=1)
        for substep in range(SUBSTEPS):
            lower = jnp.where(lane == 0, forced, pltpu.roll(forced, 1, 1))
            upper = jnp.where(lane == width - 1, forced, pltpu.roll(forced, fields * width - 1, 1))
            mixed = forced + coef * (lower + upper - 2.0 * forced)
            forced = dot3(inverse, mixed, ROWS)
        for field in range(fields):
            part = forced[:, field * width:(field + 1) * width]
            out_ref[:, field, cols] = jnp.where(live, part, states[field])
            restricted = dot3(part, weights_ip, ROWS)
            change_ref[g, :, field, :] = jnp.where(live, restricted - fetched_refs[g][0, :, field, :], 0.0)


def nest_step(nest_live, owner, nest_mixing, arrived, nest, relax, nest_inverse, interp, group=4):
    levels, fields, span = nest.shape
    width = interp.shape[1]
    count = span // width

    def named(g):
        return pl.BlockSpec(
            (1, levels, fields, width), lambda j, live, src: (src[j * group + g], 0, 0, 0)
        )

    grid_spec = pltpu.PrefetchScalarGridSpec(
        num_scalar_prefetch=2,
        grid=(count // group,),
        in_specs=[pl.BlockSpec(memory_space=pltpu.SMEM)]
        + [named(g) for g in range(group)]
        + [
            pl.BlockSpec((levels, fields, group * width), lambda j, live, src: (0, 0, j)),
            pl.BlockSpec((group, 1, width), lambda j, live, src: (j, 0, 0)),
            pl.BlockSpec((group, levels, levels), lambda j, live, src: (j, 0, 0)),
            pl.BlockSpec((group, width, width), lambda j, live, src: (j, 0, 0)),
        ],
        out_specs=[
            pl.BlockSpec((levels, fields, group * width), lambda j, live, src: (0, 0, j)),
            pl.BlockSpec((group, levels, fields, width), lambda j, live, src: (j, 0, 0, 0)),
        ],
    )
    return pl.pallas_call(
        nest_kernel,
        grid_spec=grid_spec,
        out_shape=[
            jax.ShapeDtypeStruct(nest.shape, jnp.float32),
            jax.ShapeDtypeStruct((count, levels, fields, width), jnp.float32),
        ],
        compiler_params=pltpu.CompilerParams(vmem_limit_bytes=48 * 1024 * 1024),
    )(nest_live, owner, nest_mixing, *([arrived] * group), nest, relax.reshape(count, 1, width), nest_inverse, interp)


def copy_kernel(index_ref, block_ref, out_ref):
    out_ref[...] = block_ref[...]


def send_blocks(index, blocks, count):
    _, levels, fields, width = blocks.shape
    grid_spec = pltpu.PrefetchScalarGridSpec(
        num_scalar_prefetch=1,
        grid=(count,),
        in_specs=[pl.BlockSpec((1, levels, fields, width), lambda g, index: (index[g], 0, 0, 0))],
        out_specs=pl.BlockSpec((1, levels, fields, width), lambda g, index: (g, 0, 0, 0)),
    )
    return pl.pallas_call(
        copy_kernel,
        grid_spec=grid_spec,
        out_shape=jax.ShapeDtypeStruct((count, levels, fields, width), jnp.float32),
    )(index, blocks)


def body(
    parent,
    parent_inverse,
    nest,
    nest_inverse,
    interp,
    relax,
    src_list,
    nest_live,
    mixing,
    nest_mixing,
):
    fields, levels, parent_cols = parent.shape
    parent_count = parent_inverse.shape[0]
    nest_count = nest_inverse.shape[0]
    width = interp.shape[1]
    group = lax.axis_size("sub")

    parent_lf = jnp.transpose(parent, (1, 0, 2))
    padded = with_halo(parent_lf, ((("tile", "sub"), 2),), 1)
    smoothed = parent_lf + mixing[None, :, None] * (
        padded[:, :, :-2] + padded[:, :, 2:] - 2.0 * parent_lf
    )

    owner = src_list // parent_count
    local = src_list % parent_count
    peers = jnp.arange(group, dtype=jnp.int32)
    named = owner[None, :] == peers[:, None]
    want = jnp.max(jnp.where(named, local[None, :], -1), axis=1)
    wanted = lax.all_to_all(want, "sub", split_axis=0, concat_axis=0, tiled=True)
    send_index = jnp.maximum(wanted, 0)
    gather_back = named.astype(jnp.float32)
    blocks = jnp.arange(parent_count, dtype=jnp.int32)
    place = (wanted[None, :] == blocks[:, None]).astype(jnp.float32)

    shaped = smoothed.reshape(levels, fields, parent_count, width)
    stepped = jnp.einsum("klm,mfkc->klfc", parent_inverse, shaped, precision=HIGH)
    outgoing = send_blocks(send_index, stepped, group)
    arrived = lax.all_to_all(outgoing, "sub", split_axis=0, concat_axis=0, tiled=True)

    nest_lf = jnp.transpose(nest, (1, 0, 2))
    nest_out, change = nest_step(nest_live, owner, nest_mixing, arrived, nest_lf, relax, nest_inverse, interp)

    returning = jnp.einsum("oj,jlfc->olfc", gather_back, change, precision=HIGH)
    landed = lax.all_to_all(returning, "sub", split_axis=0, concat_axis=0, tiled=True)
    summed = jnp.einsum("kg,glfc->klfc", place, landed, precision=HIGH)
    parent_out = stepped + FEEDBACK * summed
    parent_out = jnp.transpose(parent_out, (2, 1, 0, 3)).reshape(fields, levels, parent_cols)
    return parent_out, jnp.transpose(nest_out, (1, 0, 2))


def solution(mesh):
    cols = P(None, None, ("tile", "sub"))
    rows = P(("tile", "sub"), None, None)
    flat = P(("tile", "sub"))
    in_specs = (cols, rows, cols, rows, rows, flat, flat, flat, P(), P())
    out_specs = (cols, cols)
    return jax.shard_map(body, mesh=mesh, in_specs=in_specs, out_specs=out_specs, check_vma=False)
```

```python
import jax
import jax.numpy as jnp
from jax import lax
from jax.experimental import pallas as pl
from jax.experimental.pallas import tpu as pltpu
from jax.sharding import PartitionSpec as P

SUBSTEPS = 3


FEEDBACK = 0.25

HIGH = lax.Precision.HIGHEST


def with_halo(block, sides, width):
    for axis, dim in sides:
        count = lax.axis_size(axis)
        forward = [(i, i + 1) for i in range(count - 1)]
        forward.append((count - 1, 0))
        backward = [(target, source) for source, target in forward]
        low = lax.ppermute(
            lax.slice_in_dim(block, block.shape[dim] - width, None, axis=dim), axis, forward
        )
        high = lax.ppermute(lax.slice_in_dim(block, 0, width, axis=dim), axis, backward)
        block = jnp.concatenate([low, block, high], axis=dim)
    return block


def dot3(a, b, dims):
    ah = a.astype(jnp.bfloat16)
    al = (a - ah.astype(jnp.float32)).astype(jnp.bfloat16)
    bh = b.astype(jnp.bfloat16)
    bl = (b - bh.astype(jnp.float32)).astype(jnp.bfloat16)
    f = lambda x, y: lax.dot_general(x, y, dims, preferred_element_type=jnp.float32)
    return f(ah, bh) + (f(ah, bl) + f(al, bh))

ROWS = (((1,), (0,)), ((), ()))
COLS = (((1,), (1,)), ((), ()))

def nest_kernel(live_ref, owner_ref, coef_ref, *refs):
    *fetched_refs, nest_ref, relax_ref, inv_ref, interp_ref, out_ref, change_ref = refs
    group = len(fetched_refs)
    _, levels, fields, width = fetched_refs[0].shape
    lane = lax.broadcasted_iota(jnp.int32, (levels, fields * width), 1) % width
    coef = jnp.concatenate(
        [jnp.full((1, width), coef_ref[field], jnp.float32) for field in range(fields)], axis=1
    )
    for g in range(group):
        live = live_ref[pl.program_id(0) * group + g] == 1
        cols = slice(g * width, (g + 1) * width)
        weights = relax_ref[g]
        inverse = inv_ref[g]
        weights_ip = interp_ref[g]
        states = []
        forced = []
        for field in range(fields):
            state = nest_ref[:, field, cols]
            boundary = dot3(fetched_refs[g][0, :, field, :], weights_ip, COLS)
            states.append(state)
            forced.append(state + weights * (boundary - state))
        forced = jnp.concatenate(forced, axis=1)
        for substep in range(SUBSTEPS):
            lower = jnp.where(lane == 0, forced, pltpu.roll(forced, 1, 1))
            upper = jnp.where(lane == width - 1, forced, pltpu.roll(forced, fields * width - 1, 1))
            mixed = forced + coef * (lower + upper - 2.0 * forced)
            forced = dot3(inverse, mixed, ROWS)
        for field in range(fields):
            part = forced[:, field * width:(field + 1) * width]
            out_ref[:, field, cols] = jnp.where(live, part, states[field])
            restricted = dot3(part, weights_ip, ROWS)
            change_ref[g, :, field, :] = jnp.where(live, restricted - fetched_refs[g][0, :, field, :], 0.0)


def nest_step(nest_live, owner, nest_mixing, arrived, nest, relax, nest_inverse, interp, group=4):
    levels, fields, span = nest.shape
    width = interp.shape[1]
    count = span // width

    def named(g):
        return pl.BlockSpec(
            (1, levels, fields, width), lambda j, live, src: (src[j * group + g], 0, 0, 0)
        )

    grid_spec = pltpu.PrefetchScalarGridSpec(
        num_scalar_prefetch=2,
        grid=(count // group,),
        in_specs=[pl.BlockSpec(memory_space=pltpu.SMEM)]
        + [named(g) for g in range(group)]
        + [
            pl.BlockSpec((levels, fields, group * width), lambda j, live, src: (0, 0, j)),
            pl.BlockSpec((group, 1, width), lambda j, live, src: (j, 0, 0)),
            pl.BlockSpec((group, levels, levels), lambda j, live, src: (j, 0, 0)),
            pl.BlockSpec((group, width, width), lambda j, live, src: (j, 0, 0)),
        ],
        out_specs=[
            pl.BlockSpec((levels, fields, group * width), lambda j, live, src: (0, 0, j)),
            pl.BlockSpec((group, levels, fields, width), lambda j, live, src: (j, 0, 0, 0)),
        ],
    )
    return pl.pallas_call(
        nest_kernel,
        grid_spec=grid_spec,
        out_shape=[
            jax.ShapeDtypeStruct(nest.shape, jnp.float32),
            jax.ShapeDtypeStruct((count, levels, fields, width), jnp.float32),
        ],
        compiler_params=pltpu.CompilerParams(vmem_limit_bytes=48 * 1024 * 1024),
    )(nest_live, owner, nest_mixing, *([arrived] * group), nest, relax.reshape(count, 1, width), nest_inverse, interp)


def body(
    parent,
    parent_inverse,
    nest,
    nest_inverse,
    interp,
    relax,
    src_list,
    nest_live,
    mixing,
    nest_mixing,
):
    fields, levels, parent_cols = parent.shape
    parent_count = parent_inverse.shape[0]
    nest_count = nest_inverse.shape[0]
    width = interp.shape[1]
    group = lax.axis_size("sub")

    parent_lf = jnp.transpose(parent, (1, 0, 2))
    padded = with_halo(parent_lf, ((("tile", "sub"), 2),), 1)
    smoothed = parent_lf + mixing[None, :, None] * (
        padded[:, :, :-2] + padded[:, :, 2:] - 2.0 * parent_lf
    )

    owner = src_list // parent_count
    local = src_list % parent_count
    peers = jnp.arange(group, dtype=jnp.int32)
    named = owner[None, :] == peers[:, None]
    want = jnp.max(jnp.where(named, local[None, :], -1), axis=1)
    wanted = lax.all_to_all(want, "sub", split_axis=0, concat_axis=0, tiled=True)
    send_index = jnp.maximum(wanted, 0)
    blocks = jnp.arange(parent_count, dtype=jnp.int32)
    place = (wanted[None, :] == blocks[:, None]).astype(jnp.float32)

    shaped = smoothed.reshape(levels, fields, parent_count, width)
    stepped = jnp.einsum("klm,mfkc->klfc", parent_inverse, shaped, precision=HIGH)
    outgoing = sum(
        jnp.where((send_index == k)[:, None, None, None], stepped[k][None], 0.0)
        for k in range(parent_count)
    )
    arrived = lax.all_to_all(outgoing, "sub", split_axis=0, concat_axis=0, tiled=True)

    nest_lf = jnp.transpose(nest, (1, 0, 2))
    nest_out, change = nest_step(nest_live, owner, nest_mixing, arrived, nest_lf, relax, nest_inverse, interp)

    returning = jnp.zeros((group,) + change.shape[1:], jnp.float32).at[owner].add(change, mode="promise_in_bounds")
    landed = lax.all_to_all(returning, "sub", split_axis=0, concat_axis=0, tiled=True)
    summed = jnp.einsum("kg,glfc->klfc", place, landed, precision=HIGH)
    parent_out = stepped + FEEDBACK * summed
    parent_out = jnp.transpose(parent_out, (2, 1, 0, 3)).reshape(fields, levels, parent_cols)
    return parent_out, jnp.transpose(nest_out, (1, 0, 2))


def solution(mesh):
    cols = P(None, None, ("tile", "sub"))
    rows = P(("tile", "sub"), None, None)
    flat = P(("tile", "sub"))
    in_specs = (cols, rows, cols, rows, rows, flat, flat, flat, P(), P())
    out_specs = (cols, cols)
    return jax.shard_map(body, mesh=mesh, in_specs=in_specs, out_specs=out_specs, check_vma=False)
```
